512 devices in a mesh: gy: 4 (over x_lo, core), gz: 128 (over y, x_hi, z).
Axes of the slice: x: 4 (x_hi: 2, x_lo: 2; x = x_hi * 2 + x_lo), y: 4, z: 16, core: 2. Of those that a mesh axis runs over, the one named last changes fastest.
Arguments:
- fields: float32 [2, 3, 2, 1024, 2048], P(None, None, None, 'gz', 'gy'), may hold values from -6 to 6
- eigenstrain: float32 [3, 6], replicated, may hold values from -3 to 3
- moduli: float32 [3], replicated, may hold values from 0.6 to 2.6, as said below
Outputs:
- driving: float32 [2, 3, 2, 1024, 2048], P(None, None, None, 'gz', 'gy')
The draws below stay inside these ranges and needn't reach their ends.
Inputs may be any that keep to these rules, and one draw needn't show every extreme that they name: moduli = (C11, C12, C44) with C11 in 2.0 to 2.6, C12 in 0.9 to 1.3, C44 in 0.6 to 1.0.
All inputs are finite; a program needn't handle non-finite values.
Results may differ from the reference program's by a relative error of at most 0.0003.
Values sent between devices are 32-bit elements; how exact they have to be, the bound alone decides.
No kernel may reach another device: no remote copies, remote signals or barrier semaphores. Data moves between devices by JAX's collectives and lax.ppermute only.
A program may use at most 64 MiB of HBM per device.

```python
import jax
import jax.numpy as jnp
from jax import lax

NX = 2048
NY = 2048
NZ = 1024
VARIANTS = 3
KX = 2


def draw_moduli(key, part):
    base = jnp.array([2.0, 0.9, 0.6], jnp.float32)
    span = jnp.array([0.6, 0.4, 0.4], jnp.float32)
    return base + span * jax.random.uniform(key, (3,), jnp.float32)


def shard_levels(rng, shape, split, low, top_value):
    level = 1.0
    for position, shards_of in split:
        draws = jax.random.uniform(jax.random.fold_in(jax.random.fold_in(rng, 6), position), (shards_of,), jnp.float32, low / len(split), top_value / len(split))
        level = level * jnp.repeat(jnp.exp(draws), shape[position] // shards_of).reshape((-1,) + (1,) * (len(shape) - 1 - position))
    return level


def centred(own_key, extent, deviation, limit, pieces=(), kind=jnp.bfloat16):
    loudness = shard_levels(own_key, extent, pieces, -0.22, 0.18) if pieces else 1.0
    drawn = jax.random.normal(own_key, extent, jnp.float32) * deviation * loudness
    return jnp.minimum(jnp.maximum(drawn, -limit), limit).astype(kind)


def setup_inputs(seed: int = 0) -> dict:
    key_of = jax.random.split(jax.random.key(seed), 4)
    fields = centred(key_of[0], (2, VARIANTS, KX, NZ, NY), 1.0, 6.0, ((3, 128), (4, 4)), jnp.float32)
    eigenstrain = centred(key_of[1], (VARIANTS, 6), 0.5, 3.0, (), jnp.float32)
    moduli = draw_moduli(jax.random.fold_in(key_of[3], 71), 0)
    return {"fields": fields, "eigenstrain": eigenstrain, "moduli": moduli}


def signed_wave(index, length):
    return jnp.where(index < length // 2, index, index - length).astype(jnp.float32) / length

def voigt_tensor(entries):
    return [[entries[0], entries[5], entries[4]], [entries[5], entries[1], entries[3]], [entries[4], entries[3], entries[2]]]

def kernel_rows(kx_wave, ky_wave, kz_wave, eigenstrain, moduli):
    stiff_a = moduli[0]
    stiff_b = moduli[1]
    shear = moduli[2]
    square = kx_wave * kx_wave + ky_wave * ky_wave + kz_wave * kz_wave
    inside = square > 0.0
    inverse = lax.rsqrt(jnp.where(inside, square, 1.0))
    normal = [kx_wave * inverse, ky_wave * inverse, kz_wave * inverse]
    g_diag = [shear + (stiff_a - shear) * normal[axis_id] * normal[axis_id] for axis_id in range(3)]
    cross_coef = stiff_b + shear
    g_zero_one = cross_coef * normal[0] * normal[1]
    g_zero_two = cross_coef * normal[0] * normal[2]
    g_one_two = cross_coef * normal[1] * normal[2]
    cof_zz = g_diag[1] * g_diag[2] - g_one_two * g_one_two
    cof_zo = g_zero_two * g_one_two - g_zero_one * g_diag[2]
    cof_zt = g_zero_one * g_one_two - g_zero_two * g_diag[1]
    cof_oo = g_diag[0] * g_diag[2] - g_zero_two * g_zero_two
    cof_ot = g_zero_one * g_zero_two - g_diag[0] * g_one_two
    cof_tt = g_diag[0] * g_diag[1] - g_zero_one * g_zero_one
    determinant = g_diag[0] * cof_zz + g_zero_one * cof_zo + g_zero_two * cof_zt
    recip = 1.0 / determinant
    omega = [[cof_zz * recip, cof_zo * recip, cof_zt * recip], [cof_zo * recip, cof_oo * recip, cof_ot * recip], [cof_zt * recip, cof_ot * recip, cof_tt * recip]]
    strains = []
    stresses = []
    for variant in range(3):
        entries = [eigenstrain[variant, column] for column in range(6)]
        trace = entries[0] + entries[1] + entries[2]
        stress = [stiff_b * trace + (stiff_a - stiff_b) * entries[column] for column in range(3)]
        stress = stress + [2.0 * shear * entries[column] for column in range(3, 6)]
        strains.append(voigt_tensor(entries))
        stresses.append(voigt_tensor(stress))
    traction = []
    for variant in range(3):
        traction.append([sum((stresses[variant][first][second] * normal[second] for second in range(3))) for first in range(3)])
    response = []
    for variant in range(3):
        response.append([sum((omega[first][second] * traction[variant][second] for second in range(3))) for first in range(3)])
    kernel = []
    for source in range(3):
        kernel_row = []
        for target in range(3):
            energy = sum((stresses[source][first][second] * strains[target][first][second] for first in range(3) for second in range(3)))
            coupling = sum((traction[source][first] * response[target][first] for first in range(3)))
            kernel_row.append(jnp.where(inside, energy - coupling, 0.0))
        kernel.append(kernel_row)
    return kernel

def plane_force(index, plane, eigenstrain, moduli):
    kx_wave = index.astype(jnp.float32) / NX
    ky_wave = signed_wave(jnp.arange(NY, dtype=jnp.int32), NY)[None, :]
    kz_wave = signed_wave(jnp.arange(NZ, dtype=jnp.int32), NZ)[:, None]
    kernel = kernel_rows(kx_wave, ky_wave, kz_wave, eigenstrain, moduli)
    return jnp.stack([sum((kernel[source][target] * plane[target] for target in range(3))) for source in range(3)])

def reference(fields, eigenstrain, moduli):
    waves = fields[0] + 1j * fields[1]
    spectrum = jnp.fft.fft2(waves, axes=(2, 3))
    planes = jnp.moveaxis(spectrum, 1, 0)
    indices = jnp.arange(KX, dtype=jnp.int32)
    forced = lax.map(lambda item: plane_force(item[0], item[1], eigenstrain, moduli), (indices, planes))
    forced = jnp.moveaxis(forced, 0, 1)
    result = jnp.fft.ifft2(forced, axes=(2, 3))
    return jnp.stack([jnp.real(result), jnp.imag(result)]).astype(jnp.float32)
```

```python
import math

import jax
import jax.numpy as jnp
from jax import lax
from jax.sharding import PartitionSpec as P

NX = 2048
NY = 2048
NZ = 1024


highest = lax.Precision.HIGHEST


def partner_2(value, axis, stride):
    mask = 2**stride
    pairs = [(source, source ^ mask) for source in range(lax.axis_size(axis))]
    return lax.ppermute(value, axis, pairs)


def signed_wave(index, length):
    return jnp.where(index < length // 2, index, index - length).astype(jnp.float32) / length


def voigt_tensor(entries):
    return [
        [entries[0], entries[5], entries[4]],
        [entries[5], entries[1], entries[3]],
        [entries[4], entries[3], entries[2]],
    ]


def kernel_rows(kx_wave, ky_wave, kz_wave, eigenstrain, moduli):
    stiff_a = moduli[0]
    stiff_b = moduli[1]
    shear = moduli[2]
    square = kx_wave * kx_wave + ky_wave * ky_wave + kz_wave * kz_wave
    inside = square > 0.0
    inverse = lax.rsqrt(jnp.where(inside, square, 1.0))
    normal = [kx_wave * inverse, ky_wave * inverse, kz_wave * inverse]
    g_diag = [shear + (stiff_a - shear) * normal[axis_id] * normal[axis_id] for axis_id in range(3)]
    cross_coef = stiff_b + shear
    g_zero_one = cross_coef * normal[0] * normal[1]
    g_zero_two = cross_coef * normal[0] * normal[2]
    g_one_two = cross_coef * normal[1] * normal[2]
    cof_zz = g_diag[1] * g_diag[2] - g_one_two * g_one_two
    cof_zo = g_zero_two * g_one_two - g_zero_one * g_diag[2]
    cof_zt = g_zero_one * g_one_two - g_zero_two * g_diag[1]
    cof_oo = g_diag[0] * g_diag[2] - g_zero_two * g_zero_two
    cof_ot = g_zero_one * g_zero_two - g_diag[0] * g_one_two
    cof_tt = g_diag[0] * g_diag[1] - g_zero_one * g_zero_one
    determinant = g_diag[0] * cof_zz + g_zero_one * cof_zo + g_zero_two * cof_zt
    recip = 1.0 / determinant
    omega = [
        [cof_zz * recip, cof_zo * recip, cof_zt * recip],
        [cof_zo * recip, cof_oo * recip, cof_ot * recip],
        [cof_zt * recip, cof_ot * recip, cof_tt * recip],
    ]
    strains = []
    stresses = []
    for variant in range(3):
        entries = [eigenstrain[variant, column] for column in range(6)]
        trace = entries[0] + entries[1] + entries[2]
        stress = [stiff_b * trace + (stiff_a - stiff_b) * entries[column] for column in range(3)]
        stress = stress + [2.0 * shear * entries[column] for column in range(3, 6)]
        strains.append(voigt_tensor(entries))
        stresses.append(voigt_tensor(stress))
    traction = []
    for variant in range(3):
        traction.append(
            [
                sum((stresses[variant][first][second] * normal[second] for second in range(3)))
                for first in range(3)
            ]
        )
    response = []
    for variant in range(3):
        response.append(
            [
                sum((omega[first][second] * traction[variant][second] for second in range(3)))
                for first in range(3)
            ]
        )
    kernel = []
    for source in range(3):
        kernel_row = []
        for target in range(3):
            energy = sum(
                (
                    stresses[source][first][second] * strains[target][first][second]
                    for first in range(3)
                    for second in range(3)
                )
            )
            coupling = sum(
                (traction[source][first] * response[target][first] for first in range(3))
            )
            kernel_row.append(jnp.where(inside, energy - coupling, 0.0))
        kernel.append(kernel_row)
    return kernel


def cos_sin(numer, length):
    angle = (2.0 * math.pi / length) * (numer % length).astype(jnp.float32)
    return (jnp.cos(angle), jnp.sin(angle))


def stacked_table(length, axis):
    rows_idx = lax.broadcasted_iota(jnp.int32, (length, length), 0)
    cols_idx = lax.broadcasted_iota(jnp.int32, (length, length), 1)
    cosine, sine = cos_sin(rows_idx * cols_idx, length)
    return jnp.concatenate([cosine, sine], axis=axis)


def block_dft8(inverse):
    size = 192
    rows_idx = lax.broadcasted_iota(jnp.int32, (size, size), 0)
    cols_idx = lax.broadcasted_iota(jnp.int32, (size, size), 1)
    same = (rows_idx // 32 == cols_idx // 32) & (rows_idx % 4 == cols_idx % 4)
    cosine, sine = cos_sin(((rows_idx // 4) % 8) * ((cols_idx // 4) % 8), 8)
    cosine = jnp.where(same, cosine, 0.0)
    sine = jnp.where(same, sine, 0.0)
    if inverse:
        top = jnp.concatenate([cosine, sine], axis=1)
        bottom = jnp.concatenate([-sine, cosine], axis=1)
    else:
        top = jnp.concatenate([cosine, -sine], axis=1)
        bottom = jnp.concatenate([sine, cosine], axis=1)
    return jnp.concatenate([top, bottom], axis=0)


def matmul(spec, left, right):
    return jnp.einsum(spec, left, right, precision=highest)


def combine_rows(product, sign):
    c_re = product[:128, :192]
    c_im = product[:128, 192:]
    s_re = product[128:, :192]
    s_im = product[128:, 192:]
    if sign < 0:
        return (c_re + s_im, c_im - s_re)
    return (c_re - s_im, c_im + s_re)


def twiddle(values, factor_cos, factor_sin):
    real_part = values[0] * factor_cos - values[1] * factor_sin
    imag_part = values[1] * factor_cos + values[0] * factor_sin
    return jnp.stack([real_part, imag_part])


def rotate_neg(values):
    return jnp.stack([values[1], -values[0]])


def rotate_pos(values):
    return jnp.stack([-values[1], values[0]])


def times_i(re, im, sign):
    return (-sign * im, sign * re)


def dft4(parts, sign):
    (r0, i0), (r1, i1), (r2, i2), (r3, i3) = parts
    ar, ai = r0 + r2, i0 + i2
    br, bi = r0 - r2, i0 - i2
    cr, ci = r1 + r3, i1 + i3
    dr, di = times_i(r1 - r3, i1 - i3, sign)
    return [(ar + cr, ai + ci), (br + dr, bi + di), (ar - cr, ai - ci), (br - dr, bi - di)]


def y_forward(spectral):
    parts = [(spectral[0, ..., 128 * a:128 * a + 128], spectral[1, ..., 128 * a:128 * a + 128]) for a in range(4)]
    mixed = dft4(parts, -1)
    lanes = lax.broadcasted_iota(jnp.int32, (128,), 0)
    out = []
    for k1 in range(4):
        tw_cos, tw_sin = cos_sin(lanes * k1, 512)
        re, im = mixed[k1]
        out.append(jnp.stack([re * tw_cos + im * tw_sin, im * tw_cos - re * tw_sin]))
    stacked = jnp.stack(out, axis=-2).reshape(384, 128)
    product = matmul("kb,rb->kr", stacked_table(128, 0), stacked)
    re, im = combine_rows(product, -1)
    return jnp.concatenate([re, im], axis=1)


def y_inverse(returned):
    product = matmul("kr,kb->rb", returned, stacked_table(128, 1))
    c_re = product[:192, :128]
    s_re = product[:192, 128:]
    c_im = product[192:, :128]
    s_im = product[192:, 128:]
    re = (c_re - s_im).reshape(3, 2, 8, 4, 128)
    im = (c_im + s_re).reshape(3, 2, 8, 4, 128)
    lanes = lax.broadcasted_iota(jnp.int32, (128,), 0)
    parts = []
    for k1 in range(4):
        tw_cos, tw_sin = cos_sin(lanes * k1, 512)
        r = re[..., k1, :]
        i = im[..., k1, :]
        parts.append((r * tw_cos - i * tw_sin, i * tw_cos + r * tw_sin))
    mixed = dft4(parts, 1)
    real_part = jnp.concatenate([m[0] for m in mixed], axis=-1)
    imag_part = jnp.concatenate([m[1] for m in mixed], axis=-1)
    return jnp.stack([real_part, imag_part])


def z_twiddle(re, im, sign):
    rows_idx = lax.broadcasted_iota(jnp.int32, (128, 192), 0)
    cols_idx = lax.broadcasted_iota(jnp.int32, (128, 192), 1)
    tw_cos, tw_sin = cos_sin(rows_idx * ((cols_idx // 4) % 8), 1024)
    tw_sin = sign * tw_sin
    return jnp.concatenate([re * tw_cos - im * tw_sin, im * tw_cos + re * tw_sin], axis=1)


def shards(fields, eigenstrain, moduli):
    gy_count = lax.axis_size("gy")
    gy_index = lax.axis_index("gy")
    gz_index = lax.axis_index("gz")
    low_bit = gy_index % 2
    high_bit = gy_index // 2
    y_local = fields.shape[4]
    positions = lax.broadcasted_iota(jnp.int32, (y_local,), 0)
    partner = partner_2(fields, "gy", 1)
    halves = jnp.where(high_bit == 1, partner - fields, fields + partner)
    halves = jnp.where(high_bit * low_bit == 1, rotate_neg(halves), halves)
    partner = partner_2(halves, "gy", 0)
    spectral = jnp.where(low_bit == 1, partner - halves, halves + partner)
    residue = 2 * low_bit + high_bit
    angle = 2.0 * math.pi / NY * (positions * residue % NY).astype(jnp.float32)
    phase_cos = jnp.cos(angle)
    phase_sin = jnp.sin(angle)
    spectral = twiddle(spectral, phase_cos, -phase_sin)
    slabs = y_forward(spectral)
    pencils = lax.all_to_all(slabs, "gz", split_axis=0, concat_axis=0, tiled=True)
    table = stacked_table(128, 0)
    re, im = combine_rows(matmul("kg,gc->kc", table, pencils), -1)
    spectrum = jnp.dot(z_twiddle(re, im, -1), block_dft8(False), precision=highest)
    rows_idx = lax.broadcasted_iota(jnp.int32, (128, 64), 0)
    cols_idx = lax.broadcasted_iota(jnp.int32, (128, 64), 1)
    plane = cols_idx // 32
    kz_index = rows_idx + 128 * ((cols_idx // 4) % 8)
    ky_index = residue + gy_count * (cols_idx % 4 + 4 * gz_index)
    kx_wave = plane.astype(jnp.float32) / NX
    ky_wave = signed_wave(ky_index, NY)
    kz_wave = signed_wave(kz_index, NZ)
    kernel = kernel_rows(kx_wave, ky_wave, kz_wave, eigenstrain, moduli)
    scale = 1.0 / (NY * NZ)
    spec = spectrum.reshape(128, 2, 3, 64)
    forced = jnp.stack(
        [
            jnp.stack(
                [
                    sum((kernel[source][target] * spec[:, part, target] for target in range(3))) * scale
                    for source in range(3)
                ],
                axis=1,
            )
            for part in range(2)
        ],
        axis=1,
    ).reshape(128, 384)
    back = jnp.dot(forced, block_dft8(True), precision=highest)
    back = z_twiddle(back[:, :192], back[:, 192:], 1)
    re, im = combine_rows(matmul("kg,gc->kc", table, back), 1)
    back = jnp.concatenate([re, im], axis=1)
    returned = lax.all_to_all(back, "gz", split_axis=0, concat_axis=0, tiled=True)
    spatial = y_inverse(returned)
    spatial = twiddle(spatial, phase_cos, phase_sin)
    partner = partner_2(spatial, "gy", 0)
    halves = jnp.where(low_bit == 1, partner - spatial, spatial + partner)
    halves = jnp.where(high_bit * low_bit == 1, rotate_pos(halves), halves)
    partner = partner_2(halves, "gy", 1)
    result = jnp.where(high_bit == 1, partner - halves, halves + partner)
    return result


def solution(mesh):
    in_specs = (P(None, None, None, "gz", "gy"), P(), P())
    out_specs = P(None, None, None, "gz", "gy")
    return jax.shard_map(shards, mesh=mesh, in_specs=in_specs, out_specs=out_specs, check_vma=False)
```

```python
import math

import jax
import jax.numpy as jnp
from jax import lax
from jax.sharding import PartitionSpec as P

NX = 2048
NY = 2048
NZ = 1024


highest = lax.Precision.HIGHEST


def partner_2(value, axis, stride):
    mask = 2**stride
    pairs = [(source, source ^ mask) for source in range(lax.axis_size(axis))]
    return lax.ppermute(value, axis, pairs)


def signed_wave(index, length):
    return jnp.where(index < length // 2, index, index - length).astype(jnp.float32) / length


def kernel_rows(kx_wave, ky_wave, kz_wave, eigenstrain, moduli):
    constants = moduli.reshape(3, 1, 1)
    stiff_a = constants[0]
    stiff_b = constants[1]
    shear = constants[2]
    strain = eigenstrain
    trace = strain[:, 0:1] + strain[:, 1:2] + strain[:, 2:3]
    stress = jnp.concatenate(
        [
            moduli[1:2] * trace + (moduli[0:1] - moduli[1:2]) * strain[:, 0:3],
            2.0 * moduli[2:3] * strain[:, 3:6],
        ],
        axis=1,
    )
    voigt = [[0, 5, 4], [5, 1, 3], [4, 3, 2]]
    energy = sum(
        (
            stress[:, None, voigt[first][second]] * strain[None, :, voigt[first][second]]
            for first in range(3)
            for second in range(3)
        )
    ).reshape(3, 3, 1, 1)
    stress_b = stress.reshape(3, 6, 1, 1)
    square = kx_wave * kx_wave + ky_wave * ky_wave + kz_wave * kz_wave
    inside = square > 0.0
    inverse = lax.rsqrt(jnp.where(inside, square, 1.0))
    normal = [kx_wave * inverse, ky_wave * inverse, kz_wave * inverse]
    g_diag = [shear + (stiff_a - shear) * normal[axis_id] * normal[axis_id] for axis_id in range(3)]
    cross_coef = stiff_b + shear
    g_zero_one = cross_coef * normal[0] * normal[1]
    g_zero_two = cross_coef * normal[0] * normal[2]
    g_one_two = cross_coef * normal[1] * normal[2]
    cof_zz = g_diag[1] * g_diag[2] - g_one_two * g_one_two
    cof_zo = g_zero_two * g_one_two - g_zero_one * g_diag[2]
    cof_zt = g_zero_one * g_one_two - g_zero_two * g_diag[1]
    cof_oo = g_diag[0] * g_diag[2] - g_zero_two * g_zero_two
    cof_ot = g_zero_one * g_zero_two - g_diag[0] * g_one_two
    cof_tt = g_diag[0] * g_diag[1] - g_zero_one * g_zero_one
    determinant = g_diag[0] * cof_zz + g_zero_one * cof_zo + g_zero_two * cof_zt
    recip = 1.0 / determinant
    omega = [
        [cof_zz * recip, cof_zo * recip, cof_zt * recip],
        [cof_zo * recip, cof_oo * recip, cof_ot * recip],
        [cof_zt * recip, cof_ot * recip, cof_tt * recip],
    ]
    traction = []
    for variant in range(3):
        traction.append(
            [
                sum((stress_b[variant, voigt[first][second]] * normal[second] for second in range(3)))
                for first in range(3)
            ]
        )
    response = []
    for variant in range(3):
        response.append(
            [
                sum((omega[first][second] * traction[variant][second] for second in range(3)))
                for first in range(3)
            ]
        )
    kernel = []
    for source in range(3):
        kernel_row = []
        for target in range(3):
            coupling = sum(
                (traction[source][first] * response[target][first] for first in range(3))
            )
            kernel_row.append(jnp.where(inside, energy[source, target] - coupling, 0.0))
        kernel.append(kernel_row)
    return kernel


def cos_sin(numer, length):
    angle = (2.0 * math.pi / length) * (numer % length).astype(jnp.float32)
    return (jnp.cos(angle), jnp.sin(angle))


def stacked_table(length, axis):
    rows_idx = lax.broadcasted_iota(jnp.int32, (length, length), 0)
    cols_idx = lax.broadcasted_iota(jnp.int32, (length, length), 1)
    cosine, sine = cos_sin(rows_idx * cols_idx, length)
    return jnp.concatenate([cosine, sine], axis=axis)


def block_dft8(inverse):
    size = 192
    rows_idx = lax.broadcasted_iota(jnp.int32, (size, size), 0)
    cols_idx = lax.broadcasted_iota(jnp.int32, (size, size), 1)
    same = (rows_idx // 32 == cols_idx // 32) & (rows_idx % 4 == cols_idx % 4)
    cosine, sine = cos_sin(((rows_idx // 4) % 8) * ((cols_idx // 4) % 8), 8)
    cosine = jnp.where(same, cosine, 0.0)
    sine = jnp.where(same, sine, 0.0)
    if inverse:
        top = jnp.concatenate([cosine, sine], axis=1)
        bottom = jnp.concatenate([-sine, cosine], axis=1)
    else:
        top = jnp.concatenate([cosine, -sine], axis=1)
        bottom = jnp.concatenate([sine, cosine], axis=1)
    return jnp.concatenate([top, bottom], axis=0)


def matmul(spec, left, right):
    return jnp.einsum(spec, left, right, precision=highest)


def combine_rows(product, sign):
    c_re = product[:128, :192]
    c_im = product[:128, 192:]
    s_re = product[128:, :192]
    s_im = product[128:, 192:]
    if sign < 0:
        return (c_re + s_im, c_im - s_re)
    return (c_re - s_im, c_im + s_re)


def twiddle(values, factor_cos, factor_sin):
    real_part = values[0] * factor_cos - values[1] * factor_sin
    imag_part = values[1] * factor_cos + values[0] * factor_sin
    return jnp.stack([real_part, imag_part])


def rotate_neg(values):
    return jnp.stack([values[1], -values[0]])


def rotate_pos(values):
    return jnp.stack([-values[1], values[0]])


def times_i(re, im, sign):
    return (-sign * im, sign * re)


def dft4(parts, sign):
    (r0, i0), (r1, i1), (r2, i2), (r3, i3) = parts
    ar, ai = r0 + r2, i0 + i2
    br, bi = r0 - r2, i0 - i2
    cr, ci = r1 + r3, i1 + i3
    dr, di = times_i(r1 - r3, i1 - i3, sign)
    return [(ar + cr, ai + ci), (br + dr, bi + di), (ar - cr, ai - ci), (br - dr, bi - di)]


def y_forward(spectral):
    parts = [(spectral[0, ..., 128 * a:128 * a + 128], spectral[1, ..., 128 * a:128 * a + 128]) for a in range(4)]
    mixed = dft4(parts, -1)
    lanes = lax.broadcasted_iota(jnp.int32, (128,), 0)
    out = []
    for k1 in range(4):
        tw_cos, tw_sin = cos_sin(lanes * k1, 512)
        re, im = mixed[k1]
        out.append(jnp.stack([re * tw_cos + im * tw_sin, im * tw_cos - re * tw_sin]))
    stacked = jnp.stack(out, axis=-2).reshape(384, 128)
    product = matmul("kb,rb->kr", stacked_table(128, 0), stacked)
    re, im = combine_rows(product, -1)
    return jnp.concatenate([re, im], axis=1)


def y_inverse(returned):
    product = matmul("kr,kb->rb", returned, stacked_table(128, 1))
    c_re = product[:192, :128]
    s_re = product[:192, 128:]
    c_im = product[192:, :128]
    s_im = product[192:, 128:]
    re = (c_re - s_im).reshape(3, 2, 8, 4, 128)
    im = (c_im + s_re).reshape(3, 2, 8, 4, 128)
    lanes = lax.broadcasted_iota(jnp.int32, (128,), 0)
    parts = []
    for k1 in range(4):
        tw_cos, tw_sin = cos_sin(lanes * k1, 512)
        r = re[..., k1, :]
        i = im[..., k1, :]
        parts.append((r * tw_cos - i * tw_sin, i * tw_cos + r * tw_sin))
    mixed = dft4(parts, 1)
    real_part = jnp.concatenate([m[0] for m in mixed], axis=-1)
    imag_part = jnp.concatenate([m[1] for m in mixed], axis=-1)
    return jnp.stack([real_part, imag_part])


def z_twiddle(re, im, sign):
    rows_idx = lax.broadcasted_iota(jnp.int32, (128, 192), 0)
    cols_idx = lax.broadcasted_iota(jnp.int32, (128, 192), 1)
    tw_cos, tw_sin = cos_sin(rows_idx * ((cols_idx // 4) % 8), 1024)
    tw_sin = sign * tw_sin
    return jnp.concatenate([re * tw_cos - im * tw_sin, im * tw_cos + re * tw_sin], axis=1)


def shards(fields, eigenstrain, moduli):
    gy_count = lax.axis_size("gy")
    gy_index = lax.axis_index("gy")
    gz_index = lax.axis_index("gz")
    low_bit = lax.rem(gy_index, 2)
    high_bit = lax.div(gy_index, 2)
    y_local = fields.shape[4]
    positions = lax.broadcasted_iota(jnp.int32, (y_local,), 0)
    partner = partner_2(fields, "gy", 1)
    halves = jnp.where(high_bit == 1, partner - fields, fields + partner)
    halves = jnp.where(high_bit * low_bit == 1, rotate_neg(halves), halves)
    partner = partner_2(halves, "gy", 0)
    spectral = jnp.where(low_bit == 1, partner - halves, halves + partner)
    residue = 2 * low_bit + high_bit
    angle = 2.0 * math.pi / NY * (positions * residue % NY).astype(jnp.float32)
    phase_cos = jnp.cos(angle)
    phase_sin = jnp.sin(angle)
    spectral = twiddle(spectral, phase_cos, -phase_sin)
    slabs = y_forward(spectral)
    pencils = lax.all_to_all(slabs, "gz", split_axis=0, concat_axis=0, tiled=True)
    table = stacked_table(128, 0)
    re, im = combine_rows(matmul("kg,gc->kc", table, pencils), -1)
    spectrum = jnp.dot(z_twiddle(re, im, -1), block_dft8(False), precision=highest)
    rows_idx = lax.broadcasted_iota(jnp.int32, (128, 64), 0)
    cols_idx = lax.broadcasted_iota(jnp.int32, (128, 64), 1)
    plane = cols_idx // 32
    kz_index = rows_idx + 128 * ((cols_idx // 4) % 8)
    ky_index = residue + gy_count * (cols_idx % 4 + 4 * gz_index)
    kx_wave = plane.astype(jnp.float32) / NX
    ky_wave = signed_wave(ky_index, NY)
    kz_wave = signed_wave(kz_index, NZ)
    kernel = kernel_rows(kx_wave, ky_wave, kz_wave, eigenstrain, moduli)
    scale = 1.0 / (NY * NZ)
    spec = spectrum.reshape(128, 2, 3, 64)
    forced = jnp.stack(
        [
            jnp.stack(
                [
                    sum((kernel[source][target] * spec[:, part, target] for target in range(3))) * scale
                    for source in range(3)
                ],
                axis=1,
            )
            for part in range(2)
        ],
        axis=1,
    ).reshape(128, 384)
    back = jnp.dot(forced, block_dft8(True), precision=highest)
    back = z_twiddle(back[:, :192], back[:, 192:], 1)
    re, im = combine_rows(matmul("kg,gc->kc", table, back), 1)
    back = jnp.concatenate([re, im], axis=1)
    returned = lax.all_to_all(back, "gz", split_axis=0, concat_axis=0, tiled=True)
    spatial = y_inverse(returned)
    spatial = twiddle(spatial, phase_cos, phase_sin)
    partner = partner_2(spatial, "gy", 0)
    halves = jnp.where(low_bit == 1, partner - spatial, spatial + partner)
    halves = jnp.where(high_bit * low_bit == 1, rotate_pos(halves), halves)
    partner = partner_2(halves, "gy", 1)
    result = jnp.where(high_bit == 1, partner - halves, halves + partner)
    return result


def solution(mesh):
    in_specs = (P(None, None, None, "gz", "gy"), P(), P())
    out_specs = P(None, None, None, "gz", "gy")
    return jax.shard_map(shards, mesh=mesh, in_specs=in_specs, out_specs=out_specs, check_vma=False)
```

```python
import math

import jax
import jax.numpy as jnp
from jax import lax
from jax.sharding import PartitionSpec as P

NX = 2048
NY = 2048
NZ = 1024


highest = lax.Precision.HIGHEST


def partner_2(value, axis, stride):
    mask = 2**stride
    pairs = [(source, source ^ mask) for source in range(lax.axis_size(axis))]
    return lax.ppermute(value, axis, pairs)


def signed_wave(index, length):
    return jnp.where(index < length // 2, index, index - length).astype(jnp.float32) / length


def kernel_rows(kx_wave, ky_wave, kz_wave, eigenstrain, moduli):
    constants = moduli.reshape(3, 1, 1)
    stiff_a = constants[0]
    stiff_b = constants[1]
    shear = constants[2]
    strain = eigenstrain
    trace = strain[:, 0:1] + strain[:, 1:2] + strain[:, 2:3]
    stress = jnp.concatenate(
        [
            moduli[1:2] * trace + (moduli[0:1] - moduli[1:2]) * strain[:, 0:3],
            2.0 * moduli[2:3] * strain[:, 3:6],
        ],
        axis=1,
    )
    voigt = [[0, 5, 4], [5, 1, 3], [4, 3, 2]]
    energy = sum(
        (
            stress[:, None, voigt[first][second]] * strain[None, :, voigt[first][second]]
            for first in range(3)
            for second in range(3)
        )
    ).reshape(3, 3, 1, 1)
    stress_b = stress.reshape(3, 6, 1, 1)
    constants, stress_b, energy = lax.optimization_barrier((constants, stress_b, energy))
    stiff_a = constants[0]
    stiff_b = constants[1]
    shear = constants[2]
    square = kx_wave * kx_wave + ky_wave * ky_wave + kz_wave * kz_wave
    inside = square > 0.0
    inverse = lax.rsqrt(jnp.where(inside, square, 1.0))
    normal = [kx_wave * inverse, ky_wave * inverse, kz_wave * inverse]
    g_diag = [shear + (stiff_a - shear) * normal[axis_id] * normal[axis_id] for axis_id in range(3)]
    cross_coef = stiff_b + shear
    g_zero_one = cross_coef * normal[0] * normal[1]
    g_zero_two = cross_coef * normal[0] * normal[2]
    g_one_two = cross_coef * normal[1] * normal[2]
    cof_zz = g_diag[1] * g_diag[2] - g_one_two * g_one_two
    cof_zo = g_zero_two * g_one_two - g_zero_one * g_diag[2]
    cof_zt = g_zero_one * g_one_two - g_zero_two * g_diag[1]
    cof_oo = g_diag[0] * g_diag[2] - g_zero_two * g_zero_two
    cof_ot = g_zero_one * g_zero_two - g_diag[0] * g_one_two
    cof_tt = g_diag[0] * g_diag[1] - g_zero_one * g_zero_one
    determinant = g_diag[0] * cof_zz + g_zero_one * cof_zo + g_zero_two * cof_zt
    recip = 1.0 / determinant
    omega = [
        [cof_zz * recip, cof_zo * recip, cof_zt * recip],
        [cof_zo * recip, cof_oo * recip, cof_ot * recip],
        [cof_zt * recip, cof_ot * recip, cof_tt * recip],
    ]
    traction = []
    for variant in range(3):
        traction.append(
            [
                sum((stress_b[variant, voigt[first][second]] * normal[second] for second in range(3)))
                for first in range(3)
            ]
        )
    response = []
    for variant in range(3):
        response.append(
            [
                sum((omega[first][second] * traction[variant][second] for second in range(3)))
                for first in range(3)
            ]
        )
    kernel = []
    for source in range(3):
        kernel_row = []
        for target in range(3):
            coupling = sum(
                (traction[source][first] * response[target][first] for first in range(3))
            )
            kernel_row.append(jnp.where(inside, energy[source, target] - coupling, 0.0))
        kernel.append(kernel_row)
    return kernel


def cos_sin(numer, length):
    angle = (2.0 * math.pi / length) * (numer % length).astype(jnp.float32)
    return (jnp.cos(angle), jnp.sin(angle))


def stacked_table(length, axis):
    rows_idx = lax.broadcasted_iota(jnp.int32, (length, length), 0)
    cols_idx = lax.broadcasted_iota(jnp.int32, (length, length), 1)
    cosine, sine = cos_sin(rows_idx * cols_idx, length)
    return jnp.concatenate([cosine, sine], axis=axis)


def block_dft8(inverse):
    size = 192
    rows_idx = lax.broadcasted_iota(jnp.int32, (size, size), 0)
    cols_idx = lax.broadcasted_iota(jnp.int32, (size, size), 1)
    same = (rows_idx // 32 == cols_idx // 32) & (rows_idx % 4 == cols_idx % 4)
    cosine, sine = cos_sin(((rows_idx // 4) % 8) * ((cols_idx // 4) % 8), 8)
    cosine = jnp.where(same, cosine, 0.0)
    sine = jnp.where(same, sine, 0.0)
    if inverse:
        top = jnp.concatenate([cosine, sine], axis=1)
        bottom = jnp.concatenate([-sine, cosine], axis=1)
    else:
        top = jnp.concatenate([cosine, -sine], axis=1)
        bottom = jnp.concatenate([sine, cosine], axis=1)
    return jnp.concatenate([top, bottom], axis=0)


def matmul(spec, left, right):
    return jnp.einsum(spec, left, right, precision=highest)


def combine_rows(product, sign):
    c_re = product[:128, :192]
    c_im = product[:128, 192:]
    s_re = product[128:, :192]
    s_im = product[128:, 192:]
    if sign < 0:
        return (c_re + s_im, c_im - s_re)
    return (c_re - s_im, c_im + s_re)


def twiddle(values, factor_cos, factor_sin):
    real_part = values[0] * factor_cos - values[1] * factor_sin
    imag_part = values[1] * factor_cos + values[0] * factor_sin
    return jnp.stack([real_part, imag_part])


def rotate_neg(values):
    return jnp.stack([values[1], -values[0]])


def rotate_pos(values):
    return jnp.stack([-values[1], values[0]])


def times_i(re, im, sign):
    return (-sign * im, sign * re)


def dft4(parts, sign):
    (r0, i0), (r1, i1), (r2, i2), (r3, i3) = parts
    ar, ai = r0 + r2, i0 + i2
    br, bi = r0 - r2, i0 - i2
    cr, ci = r1 + r3, i1 + i3
    dr, di = times_i(r1 - r3, i1 - i3, sign)
    return [(ar + cr, ai + ci), (br + dr, bi + di), (ar - cr, ai - ci), (br - dr, bi - di)]


def y_forward(spectral):
    parts = [(spectral[0, ..., 128 * a:128 * a + 128], spectral[1, ..., 128 * a:128 * a + 128]) for a in range(4)]
    mixed = dft4(parts, -1)
    lanes = lax.broadcasted_iota(jnp.int32, (128,), 0)
    out = []
    for k1 in range(4):
        tw_cos, tw_sin = cos_sin(lanes * k1, 512)
        re, im = mixed[k1]
        out.append(jnp.stack([re * tw_cos + im * tw_sin, im * tw_cos - re * tw_sin]))
    stacked = jnp.stack(out, axis=-2).reshape(384, 128)
    product = matmul("kb,rb->kr", stacked_table(128, 0), stacked)
    re, im = combine_rows(product, -1)
    return jnp.concatenate([re, im], axis=1)


def y_inverse(returned):
    product = matmul("kr,kb->rb", returned, stacked_table(128, 1))
    c_re = product[:192, :128]
    s_re = product[:192, 128:]
    c_im = product[192:, :128]
    s_im = product[192:, 128:]
    re = (c_re - s_im).reshape(3, 2, 8, 4, 128)
    im = (c_im + s_re).reshape(3, 2, 8, 4, 128)
    lanes = lax.broadcasted_iota(jnp.int32, (128,), 0)
    parts = []
    for k1 in range(4):
        tw_cos, tw_sin = cos_sin(lanes * k1, 512)
        r = re[..., k1, :]
        i = im[..., k1, :]
        parts.append((r * tw_cos - i * tw_sin, i * tw_cos + r * tw_sin))
    mixed = dft4(parts, 1)
    real_part = jnp.concatenate([m[0] for m in mixed], axis=-1)
    imag_part = jnp.concatenate([m[1] for m in mixed], axis=-1)
    return jnp.stack([real_part, imag_part])


def z_twiddle(re, im, sign):
    rows_idx = lax.broadcasted_iota(jnp.int32, (128, 192), 0)
    cols_idx = lax.broadcasted_iota(jnp.int32, (128, 192), 1)
    tw_cos, tw_sin = cos_sin(rows_idx * ((cols_idx // 4) % 8), 1024)
    tw_sin = sign * tw_sin
    return jnp.concatenate([re * tw_cos - im * tw_sin, im * tw_cos + re * tw_sin], axis=1)


def shards(fields, eigenstrain, moduli):
    gy_count = lax.axis_size("gy")
    gy_index = lax.axis_index("gy")
    gz_index = lax.axis_index("gz")
    low_bit = lax.rem(gy_index, 2)
    high_bit = lax.div(gy_index, 2)
    y_local = fields.shape[4]
    positions = lax.broadcasted_iota(jnp.int32, (y_local,), 0)
    partner = partner_2(fields, "gy", 1)
    halves = jnp.where(high_bit == 1, partner - fields, fields + partner)
    halves = jnp.where(high_bit * low_bit == 1, rotate_neg(halves), halves)
    partner = partner_2(halves, "gy", 0)
    spectral = jnp.where(low_bit == 1, partner - halves, halves + partner)
    residue = 2 * low_bit + high_bit
    angle = 2.0 * math.pi / NY * (positions * residue % NY).astype(jnp.float32)
    phase_cos = jnp.cos(angle)
    phase_sin = jnp.sin(angle)
    spectral = twiddle(spectral, phase_cos, -phase_sin)
    slabs = y_forward(spectral)
    pencils = lax.all_to_all(slabs, "gz", split_axis=0, concat_axis=0, tiled=True)
    table = stacked_table(128, 0)
    re, im = combine_rows(matmul("kg,gc->kc", table, pencils), -1)
    spectrum = jnp.dot(z_twiddle(re, im, -1), block_dft8(False), precision=highest)
    rows_idx = lax.broadcasted_iota(jnp.int32, (128, 64), 0)
    cols_idx = lax.broadcasted_iota(jnp.int32, (128, 64), 1)
    plane = cols_idx // 32
    kz_index = rows_idx + 128 * ((cols_idx // 4) % 8)
    ky_index = residue + gy_count * (cols_idx % 4 + 4 * gz_index)
    kx_wave = plane.astype(jnp.float32) / NX
    ky_wave = signed_wave(ky_index, NY)
    kz_wave = signed_wave(kz_index, NZ)
    kernel = kernel_rows(kx_wave, ky_wave, kz_wave, eigenstrain, moduli)
    kernel = lax.optimization_barrier(jnp.stack([jnp.stack(row) for row in kernel]))
    scale = 1.0 / (NY * NZ)
    spec = spectrum.reshape(128, 2, 3, 64)
    forced = jnp.stack(
        [
            jnp.stack(
                [
                    sum((kernel[source][target] * spec[:, part, target] for target in range(3))) * scale
                    for source in range(3)
                ],
                axis=1,
            )
            for part in range(2)
        ],
        axis=1,
    ).reshape(128, 384)
    back = jnp.dot(forced, block_dft8(True), precision=highest)
    back = z_twiddle(back[:, :192], back[:, 192:], 1)
    re, im = combine_rows(matmul("kg,gc->kc", table, back), 1)
    back = jnp.concatenate([re, im], axis=1)
    returned = lax.all_to_all(back, "gz", split_axis=0, concat_axis=0, tiled=True)
    spatial = y_inverse(returned)
    spatial = twiddle(spatial, phase_cos, phase_sin)
    partner = partner_2(spatial, "gy", 0)
    halves = jnp.where(low_bit == 1, partner - spatial, spatial + partner)
    halves = jnp.where(high_bit * low_bit == 1, rotate_pos(halves), halves)
    partner = partner_2(halves, "gy", 1)
    result = jnp.where(high_bit == 1, partner - halves, halves + partner)
    return result


def solution(mesh):
    in_specs = (P(None, None, None, "gz", "gy"), P(), P())
    out_specs = P(None, None, None, "gz", "gy")
    return jax.shard_map(shards, mesh=mesh, in_specs=in_specs, out_specs=out_specs, check_vma=False)
```

```python
import math

import jax
import jax.numpy as jnp
from jax import lax
from jax.sharding import PartitionSpec as P

NX = 2048
NY = 2048
NZ = 1024


highest = lax.Precision.HIGHEST


def partner_2(value, axis, stride):
    mask = 2**stride
    pairs = [(source, source ^ mask) for source in range(lax.axis_size(axis))]
    return lax.ppermute(value, axis, pairs)


def signed_wave(index, length):
    return jnp.where(index < length // 2, index, index - length).astype(jnp.float32) / length


def kernel_rows(kx_wave, ky_wave, kz_wave, eigenstrain, moduli):
    constants = moduli.reshape(3, 1, 1)
    stiff_a = constants[0]
    stiff_b = constants[1]
    shear = constants[2]
    strain = eigenstrain
    trace = strain[:, 0:1] + strain[:, 1:2] + strain[:, 2:3]
    stress = jnp.concatenate(
        [
            moduli[1:2] * trace + (moduli[0:1] - moduli[1:2]) * strain[:, 0:3],
            2.0 * moduli[2:3] * strain[:, 3:6],
        ],
        axis=1,
    )
    voigt = [[0, 5, 4], [5, 1, 3], [4, 3, 2]]
    energy = sum(
        (
            stress[:, None, voigt[first][second]] * strain[None, :, voigt[first][second]]
            for first in range(3)
            for second in range(3)
        )
    )
    width = kx_wave.shape[-1]
    constants = jnp.broadcast_to(moduli[:, None], (3, width))
    stress_b = jnp.broadcast_to(stress[:, :, None], (3, 6, width))
    energy = jnp.broadcast_to(energy[:, :, None], (3, 3, width))
    constants, stress_b, energy = lax.optimization_barrier((constants, stress_b, energy))
    stiff_a = constants[0]
    stiff_b = constants[1]
    shear = constants[2]
    square = kx_wave * kx_wave + ky_wave * ky_wave + kz_wave * kz_wave
    inside = square > 0.0
    inverse = lax.rsqrt(jnp.where(inside, square, 1.0))
    normal = [kx_wave * inverse, ky_wave * inverse, kz_wave * inverse]
    g_diag = [shear + (stiff_a - shear) * normal[axis_id] * normal[axis_id] for axis_id in range(3)]
    cross_coef = stiff_b + shear
    g_zero_one = cross_coef * normal[0] * normal[1]
    g_zero_two = cross_coef * normal[0] * normal[2]
    g_one_two = cross_coef * normal[1] * normal[2]
    cof_zz = g_diag[1] * g_diag[2] - g_one_two * g_one_two
    cof_zo = g_zero_two * g_one_two - g_zero_one * g_diag[2]
    cof_zt = g_zero_one * g_one_two - g_zero_two * g_diag[1]
    cof_oo = g_diag[0] * g_diag[2] - g_zero_two * g_zero_two
    cof_ot = g_zero_one * g_zero_two - g_diag[0] * g_one_two
    cof_tt = g_diag[0] * g_diag[1] - g_zero_one * g_zero_one
    determinant = g_diag[0] * cof_zz + g_zero_one * cof_zo + g_zero_two * cof_zt
    recip = 1.0 / determinant
    omega = [
        [cof_zz * recip, cof_zo * recip, cof_zt * recip],
        [cof_zo * recip, cof_oo * recip, cof_ot * recip],
        [cof_zt * recip, cof_ot * recip, cof_tt * recip],
    ]
    traction = []
    for variant in range(3):
        traction.append(
            [
                sum((stress_b[variant, voigt[first][second]] * normal[second] for second in range(3)))
                for first in range(3)
            ]
        )
    response = []
    for variant in range(3):
        response.append(
            [
                sum((omega[first][second] * traction[variant][second] for second in range(3)))
                for first in range(3)
            ]
        )
    kernel = []
    for source in range(3):
        kernel_row = []
        for target in range(3):
            coupling = sum(
                (traction[source][first] * response[target][first] for first in range(3))
            )
            kernel_row.append(jnp.where(inside, energy[source, target] - coupling, 0.0))
        kernel.append(kernel_row)
    return kernel


def cos_sin(numer, length):
    angle = (2.0 * math.pi / length) * (numer % length).astype(jnp.float32)
    return (jnp.cos(angle), jnp.sin(angle))


def stacked_table(length, axis):
    rows_idx = lax.broadcasted_iota(jnp.int32, (length, length), 0)
    cols_idx = lax.broadcasted_iota(jnp.int32, (length, length), 1)
    cosine, sine = cos_sin(rows_idx * cols_idx, length)
    return jnp.concatenate([cosine, sine], axis=axis)


def block_dft8(inverse):
    size = 192
    rows_idx = lax.broadcasted_iota(jnp.int32, (size, size), 0)
    cols_idx = lax.broadcasted_iota(jnp.int32, (size, size), 1)
    same = (rows_idx // 32 == cols_idx // 32) & (rows_idx % 4 == cols_idx % 4)
    cosine, sine = cos_sin(((rows_idx // 4) % 8) * ((cols_idx // 4) % 8), 8)
    cosine = jnp.where(same, cosine, 0.0)
    sine = jnp.where(same, sine, 0.0)
    if inverse:
        top = jnp.concatenate([cosine, sine], axis=1)
        bottom = jnp.concatenate([-sine, cosine], axis=1)
    else:
        top = jnp.concatenate([cosine, -sine], axis=1)
        bottom = jnp.concatenate([sine, cosine], axis=1)
    return jnp.concatenate([top, bottom], axis=0)


def matmul(spec, left, right):
    return jnp.einsum(spec, left, right, precision=highest)


def combine_rows(product, sign):
    c_re = product[:128, :192]
    c_im = product[:128, 192:]
    s_re = product[128:, :192]
    s_im = product[128:, 192:]
    if sign < 0:
        return (c_re + s_im, c_im - s_re)
    return (c_re - s_im, c_im + s_re)


def twiddle(values, factor_cos, factor_sin):
    real_part = values[0] * factor_cos - values[1] * factor_sin
    imag_part = values[1] * factor_cos + values[0] * factor_sin
    return jnp.stack([real_part, imag_part])


def rotate_neg(values):
    return jnp.stack([values[1], -values[0]])


def rotate_pos(values):
    return jnp.stack([-values[1], values[0]])


def times_i(re, im, sign):
    return (-sign * im, sign * re)


def dft4(parts, sign):
    (r0, i0), (r1, i1), (r2, i2), (r3, i3) = parts
    ar, ai = r0 + r2, i0 + i2
    br, bi = r0 - r2, i0 - i2
    cr, ci = r1 + r3, i1 + i3
    dr, di = times_i(r1 - r3, i1 - i3, sign)
    return [(ar + cr, ai + ci), (br + dr, bi + di), (ar - cr, ai - ci), (br - dr, bi - di)]


def y_forward(spectral):
    parts = [(spectral[0, ..., 128 * a:128 * a + 128], spectral[1, ..., 128 * a:128 * a + 128]) for a in range(4)]
    mixed = dft4(parts, -1)
    lanes = lax.broadcasted_iota(jnp.int32, (128,), 0)
    out = []
    for k1 in range(4):
        tw_cos, tw_sin = cos_sin(lanes * k1, 512)
        re, im = mixed[k1]
        out.append(jnp.stack([re * tw_cos + im * tw_sin, im * tw_cos - re * tw_sin]))
    stacked = jnp.stack(out, axis=-2).reshape(384, 128)
    product = matmul("kb,rb->kr", stacked_table(128, 0), stacked)
    re, im = combine_rows(product, -1)
    return jnp.concatenate([re, im], axis=1)


def y_inverse(returned):
    product = matmul("kr,kb->rb", returned, stacked_table(128, 1))
    c_re = product[:192, :128]
    s_re = product[:192, 128:]
    c_im = product[192:, :128]
    s_im = product[192:, 128:]
    re = (c_re - s_im).reshape(3, 2, 8, 4, 128)
    im = (c_im + s_re).reshape(3, 2, 8, 4, 128)
    lanes = lax.broadcasted_iota(jnp.int32, (128,), 0)
    parts = []
    for k1 in range(4):
        tw_cos, tw_sin = cos_sin(lanes * k1, 512)
        r = re[..., k1, :]
        i = im[..., k1, :]
        parts.append((r * tw_cos - i * tw_sin, i * tw_cos + r * tw_sin))
    mixed = dft4(parts, 1)
    real_part = jnp.concatenate([m[0] for m in mixed], axis=-1)
    imag_part = jnp.concatenate([m[1] for m in mixed], axis=-1)
    return jnp.stack([real_part, imag_part])


def z_twiddle(re, im, sign):
    rows_idx = lax.broadcasted_iota(jnp.int32, (128, 192), 0)
    cols_idx = lax.broadcasted_iota(jnp.int32, (128, 192), 1)
    tw_cos, tw_sin = cos_sin(rows_idx * ((cols_idx // 4) % 8), 1024)
    tw_sin = sign * tw_sin
    return jnp.concatenate([re * tw_cos - im * tw_sin, im * tw_cos + re * tw_sin], axis=1)


def shards(fields, eigenstrain, moduli):
    gy_count = lax.axis_size("gy")
    gy_index = lax.axis_index("gy")
    gz_index = lax.axis_index("gz")
    low_bit = lax.rem(gy_index, 2)
    high_bit = lax.div(gy_index, 2)
    y_local = fields.shape[4]
    positions = lax.broadcasted_iota(jnp.int32, (y_local,), 0)
    partner = partner_2(fields, "gy", 1)
    halves = jnp.where(high_bit == 1, partner - fields, fields + partner)
    halves = jnp.where(high_bit * low_bit == 1, rotate_neg(halves), halves)
    partner = partner_2(halves, "gy", 0)
    spectral = jnp.where(low_bit == 1, partner - halves, halves + partner)
    residue = 2 * low_bit + high_bit
    angle = 2.0 * math.pi / NY * (positions * residue % NY).astype(jnp.float32)
    phase_cos = jnp.cos(angle)
    phase_sin = jnp.sin(angle)
    spectral = twiddle(spectral, phase_cos, -phase_sin)
    slabs = y_forward(spectral)
    pencils = lax.all_to_all(slabs, "gz", split_axis=0, concat_axis=0, tiled=True)
    table = stacked_table(128, 0)
    re, im = combine_rows(matmul("kg,gc->kc", table, pencils), -1)
    spectrum = jnp.dot(z_twiddle(re, im, -1), block_dft8(False), precision=highest)
    rows_idx = lax.broadcasted_iota(jnp.int32, (128, 64), 0)
    cols_idx = lax.broadcasted_iota(jnp.int32, (128, 64), 1)
    plane = cols_idx // 32
    kz_index = rows_idx + 128 * ((cols_idx // 4) % 8)
    ky_index = residue + gy_count * (cols_idx % 4 + 4 * gz_index)
    kx_wave = plane.astype(jnp.float32) / NX
    ky_wave = signed_wave(ky_index, NY)
    kz_wave = signed_wave(kz_index, NZ)
    kernel = kernel_rows(kx_wave, ky_wave, kz_wave, eigenstrain, moduli)
    scale = 1.0 / (NY * NZ)
    spec = spectrum.reshape(128, 2, 3, 64)
    forced = jnp.stack(
        [
            jnp.stack(
                [
                    sum((kernel[source][target] * spec[:, part, target] for target in range(3))) * scale
                    for source in range(3)
                ],
                axis=1,
            )
            for part in range(2)
        ],
        axis=1,
    ).reshape(128, 384)
    back = jnp.dot(forced, block_dft8(True), precision=highest)
    back = z_twiddle(back[:, :192], back[:, 192:], 1)
    re, im = combine_rows(matmul("kg,gc->kc", table, back), 1)
    back = jnp.concatenate([re, im], axis=1)
    returned = lax.all_to_all(back, "gz", split_axis=0, concat_axis=0, tiled=True)
    spatial = y_inverse(returned)
    spatial = twiddle(spatial, phase_cos, phase_sin)
    partner = partner_2(spatial, "gy", 0)
    halves = jnp.where(low_bit == 1, partner - spatial, spatial + partner)
    halves = jnp.where(high_bit * low_bit == 1, rotate_pos(halves), halves)
    partner = partner_2(halves, "gy", 1)
    result = jnp.where(high_bit == 1, partner - halves, halves + partner)
    return result


def solution(mesh):
    in_specs = (P(None, None, None, "gz", "gy"), P(), P())
    out_specs = P(None, None, None, "gz", "gy")
    return jax.shard_map(shards, mesh=mesh, in_specs=in_specs, out_specs=out_specs, check_vma=False)
```

```python
import math

import numpy as np

import jax
import jax.numpy as jnp
from jax import lax
from jax.sharding import PartitionSpec as P

NX = 2048
NY = 2048
NZ = 1024


highest = lax.Precision.HIGHEST


def partner_2(value, axis, stride):
    mask = 2**stride
    pairs = [(source, source ^ mask) for source in range(lax.axis_size(axis))]
    return lax.ppermute(value, axis, pairs)


def signed_wave(index, length):
    return jnp.where(index < length // 2, index, index - length).astype(jnp.float32) / length


def kernel_rows(kx_wave, ky_wave, kz_wave, eigenstrain, moduli):
    constants = moduli.reshape(3, 1, 1)
    stiff_a = constants[0]
    stiff_b = constants[1]
    shear = constants[2]
    strain = eigenstrain
    trace = strain[:, 0:1] + strain[:, 1:2] + strain[:, 2:3]
    stress = jnp.concatenate(
        [
            moduli[1:2] * trace + (moduli[0:1] - moduli[1:2]) * strain[:, 0:3],
            2.0 * moduli[2:3] * strain[:, 3:6],
        ],
        axis=1,
    )
    voigt = [[0, 5, 4], [5, 1, 3], [4, 3, 2]]
    energy = sum(
        (
            stress[:, None, voigt[first][second]] * strain[None, :, voigt[first][second]]
            for first in range(3)
            for second in range(3)
        )
    )
    width = kx_wave.shape[-1]
    constants = jnp.broadcast_to(moduli[:, None], (3, width))
    stress_b = jnp.broadcast_to(stress[:, :, None], (3, 6, width))
    energy = jnp.broadcast_to(energy[:, :, None], (3, 3, width))
    constants, stress_b, energy = lax.optimization_barrier((constants, stress_b, energy))
    stiff_a = constants[0]
    stiff_b = constants[1]
    shear = constants[2]
    square = kx_wave * kx_wave + ky_wave * ky_wave + kz_wave * kz_wave
    inside = square > 0.0
    inverse = lax.rsqrt(jnp.where(inside, square, 1.0))
    normal = [kx_wave * inverse, ky_wave * inverse, kz_wave * inverse]
    g_diag = [shear + (stiff_a - shear) * normal[axis_id] * normal[axis_id] for axis_id in range(3)]
    cross_coef = stiff_b + shear
    g_zero_one = cross_coef * normal[0] * normal[1]
    g_zero_two = cross_coef * normal[0] * normal[2]
    g_one_two = cross_coef * normal[1] * normal[2]
    cof_zz = g_diag[1] * g_diag[2] - g_one_two * g_one_two
    cof_zo = g_zero_two * g_one_two - g_zero_one * g_diag[2]
    cof_zt = g_zero_one * g_one_two - g_zero_two * g_diag[1]
    cof_oo = g_diag[0] * g_diag[2] - g_zero_two * g_zero_two
    cof_ot = g_zero_one * g_zero_two - g_diag[0] * g_one_two
    cof_tt = g_diag[0] * g_diag[1] - g_zero_one * g_zero_one
    determinant = g_diag[0] * cof_zz + g_zero_one * cof_zo + g_zero_two * cof_zt
    recip = 1.0 / determinant
    omega = [
        [cof_zz * recip, cof_zo * recip, cof_zt * recip],
        [cof_zo * recip, cof_oo * recip, cof_ot * recip],
        [cof_zt * recip, cof_ot * recip, cof_tt * recip],
    ]
    traction = []
    for variant in range(3):
        traction.append(
            [
                sum((stress_b[variant, voigt[first][second]] * normal[second] for second in range(3)))
                for first in range(3)
            ]
        )
    response = []
    for variant in range(3):
        response.append(
            [
                sum((omega[first][second] * traction[variant][second] for second in range(3)))
                for first in range(3)
            ]
        )
    kernel = []
    for source in range(3):
        kernel_row = []
        for target in range(3):
            coupling = sum(
                (traction[source][first] * response[target][first] for first in range(3))
            )
            kernel_row.append(jnp.where(inside, energy[source, target] - coupling, 0.0))
        kernel.append(kernel_row)
    return kernel


def cos_sin(numer, length):
    angle = (2.0 * math.pi / length) * (numer % length).astype(jnp.float32)
    return (jnp.cos(angle), jnp.sin(angle))


def np_cos_sin(numer, length):
    angle = (2.0 * np.pi / length) * (numer % length).astype(np.float64)
    return (np.cos(angle).astype(np.float32), np.sin(angle).astype(np.float32))


def stacked_table(length):
    index = np.arange(length)
    cosine, sine = np_cos_sin(np.outer(index, index), length)
    return np.concatenate([cosine, sine], axis=0)


def block_dft8():
    size = 192
    rows_idx = np.arange(size)[:, None]
    cols_idx = np.arange(size)[None, :]
    same = (rows_idx // 32 == cols_idx // 32) & (rows_idx % 4 == cols_idx % 4)
    cosine, sine = np_cos_sin(((rows_idx // 4) % 8) * ((cols_idx // 4) % 8), 8)
    cosine = np.where(same, cosine, 0.0).astype(np.float32)
    sine = np.where(same, sine, 0.0).astype(np.float32)
    top = np.concatenate([cosine, -sine], axis=1)
    bottom = np.concatenate([sine, cosine], axis=1)
    return np.concatenate([top, bottom], axis=0)


def z_twiddle_table():
    rows_idx = np.arange(128)[:, None]
    cols_idx = np.arange(192)[None, :]
    return np.stack(np_cos_sin(rows_idx * ((cols_idx // 4) % 8), 1024))


def y_twiddle_table():
    return np.stack(np_cos_sin(np.arange(4)[:, None] * np.arange(128)[None, :], 512))


def matmul(spec, left, right):
    return jnp.einsum(spec, left, right, precision=highest)


def combine_rows(product, sign):
    c_re = product[:128, :192]
    c_im = product[:128, 192:]
    s_re = product[128:, :192]
    s_im = product[128:, 192:]
    if sign < 0:
        return (c_re + s_im, c_im - s_re)
    return (c_re - s_im, c_im + s_re)


def twiddle(values, factor_cos, factor_sin):
    real_part = values[0] * factor_cos - values[1] * factor_sin
    imag_part = values[1] * factor_cos + values[0] * factor_sin
    return jnp.stack([real_part, imag_part])


def rotate_neg(values):
    return jnp.stack([values[1], -values[0]])


def rotate_pos(values):
    return jnp.stack([-values[1], values[0]])


def times_i(re, im, sign):
    return (-sign * im, sign * re)


def dft4(parts, sign):
    (r0, i0), (r1, i1), (r2, i2), (r3, i3) = parts
    ar, ai = r0 + r2, i0 + i2
    br, bi = r0 - r2, i0 - i2
    cr, ci = r1 + r3, i1 + i3
    dr, di = times_i(r1 - r3, i1 - i3, sign)
    return [(ar + cr, ai + ci), (br + dr, bi + di), (ar - cr, ai - ci), (br - dr, bi - di)]


def y_forward(spectral):
    parts = [(spectral[0, ..., 128 * a:128 * a + 128], spectral[1, ..., 128 * a:128 * a + 128]) for a in range(4)]
    mixed = dft4(parts, -1)
    table = y_twiddle_table()
    out = []
    for k1 in range(4):
        tw_cos, tw_sin = table[0, k1], table[1, k1]
        re, im = mixed[k1]
        out.append(jnp.stack([re * tw_cos + im * tw_sin, im * tw_cos - re * tw_sin]))
    stacked = jnp.stack(out, axis=-2).reshape(384, 128)
    product = matmul("kb,rb->kr", stacked_table(128), stacked)
    re, im = combine_rows(product, -1)
    return jnp.concatenate([re, im], axis=1)


def y_inverse(returned):
    product = matmul("kr,bk->rb", returned, stacked_table(128))
    c_re = product[:192, :128]
    s_re = product[:192, 128:]
    c_im = product[192:, :128]
    s_im = product[192:, 128:]
    re = (c_re - s_im).reshape(3, 2, 8, 4, 128)
    im = (c_im + s_re).reshape(3, 2, 8, 4, 128)
    table = y_twiddle_table()
    parts = []
    for k1 in range(4):
        tw_cos, tw_sin = table[0, k1], table[1, k1]
        r = re[..., k1, :]
        i = im[..., k1, :]
        parts.append((r * tw_cos - i * tw_sin, i * tw_cos + r * tw_sin))
    mixed = dft4(parts, 1)
    real_part = jnp.concatenate([m[0] for m in mixed], axis=-1)
    imag_part = jnp.concatenate([m[1] for m in mixed], axis=-1)
    return jnp.stack([real_part, imag_part])


def z_twiddle(re, im, sign):
    table = z_twiddle_table()
    tw_cos = table[0]
    tw_sin = sign * table[1]
    return jnp.concatenate([re * tw_cos - im * tw_sin, im * tw_cos + re * tw_sin], axis=1)


def shards(fields, eigenstrain, moduli):
    gy_count = lax.axis_size("gy")
    gy_index = lax.axis_index("gy")
    gz_index = lax.axis_index("gz")
    low_bit = lax.rem(gy_index, 2)
    high_bit = lax.div(gy_index, 2)
    y_local = fields.shape[4]
    positions = lax.broadcasted_iota(jnp.int32, (y_local,), 0)
    partner = partner_2(fields, "gy", 1)
    halves = jnp.where(high_bit == 1, partner - fields, fields + partner)
    halves = jnp.where(high_bit * low_bit == 1, rotate_neg(halves), halves)
    partner = partner_2(halves, "gy", 0)
    spectral = jnp.where(low_bit == 1, partner - halves, halves + partner)
    residue = 2 * low_bit + high_bit
    angle = 2.0 * math.pi / NY * (positions * residue % NY).astype(jnp.float32)
    phase_cos = jnp.cos(angle)
    phase_sin = jnp.sin(angle)
    spectral = twiddle(spectral, phase_cos, -phase_sin)
    slabs = y_forward(spectral)
    pencils = lax.all_to_all(slabs, "gz", split_axis=0, concat_axis=0, tiled=True)
    table = stacked_table(128)
    re, im = combine_rows(matmul("kg,gc->kc", table, pencils), -1)
    spectrum = jnp.dot(z_twiddle(re, im, -1), block_dft8(), precision=highest)
    rows_idx = lax.broadcasted_iota(jnp.int32, (128, 64), 0)
    cols_idx = lax.broadcasted_iota(jnp.int32, (128, 64), 1)
    plane = cols_idx // 32
    kz_index = rows_idx + 128 * ((cols_idx // 4) % 8)
    ky_index = residue + gy_count * (cols_idx % 4 + 4 * gz_index)
    kx_wave = plane.astype(jnp.float32) / NX
    ky_wave = signed_wave(ky_index, NY)
    kz_wave = signed_wave(kz_index, NZ)
    kernel = kernel_rows(kx_wave, ky_wave, kz_wave, eigenstrain, moduli)
    scale = 1.0 / (NY * NZ)
    spec = spectrum.reshape(128, 2, 3, 64)
    forced = jnp.stack(
        [
            jnp.stack(
                [
                    sum((kernel[source][target] * spec[:, part, target] for target in range(3))) * scale
                    for source in range(3)
                ],
                axis=1,
            )
            for part in range(2)
        ],
        axis=1,
    ).reshape(128, 384)
    back = matmul("kr,sr->ks", forced, block_dft8())
    back = z_twiddle(back[:, :192], back[:, 192:], 1)
    re, im = combine_rows(matmul("kg,gc->kc", table, back), 1)
    back = jnp.concatenate([re, im], axis=1)
    returned = lax.all_to_all(back, "gz", split_axis=0, concat_axis=0, tiled=True)
    spatial = y_inverse(returned)
    spatial = twiddle(spatial, phase_cos, phase_sin)
    partner = partner_2(spatial, "gy", 0)
    halves = jnp.where(low_bit == 1, partner - spatial, spatial + partner)
    halves = jnp.where(high_bit * low_bit == 1, rotate_pos(halves), halves)
    partner = partner_2(halves, "gy", 1)
    result = jnp.where(high_bit == 1, partner - halves, halves + partner)
    return result


def solution(mesh):
    in_specs = (P(None, None, None, "gz", "gy"), P(), P())
    out_specs = P(None, None, None, "gz", "gy")
    return jax.shard_map(shards, mesh=mesh, in_specs=in_specs, out_specs=out_specs, check_vma=False)
```

```python
import math

import numpy as np

import jax
import jax.numpy as jnp
from jax import lax
from jax.sharding import PartitionSpec as P

NX = 2048
NY = 2048
NZ = 1024


highest = lax.Precision.HIGHEST


def partner_2(value, axis, stride):
    mask = 2**stride
    pairs = [(source, source ^ mask) for source in range(lax.axis_size(axis))]
    return lax.ppermute(value, axis, pairs)


def signed_wave(index, length):
    return jnp.where(index < length // 2, index, index - length).astype(jnp.float32) / length


def kernel_rows(kx_wave, ky_wave, kz_wave, eigenstrain, moduli):
    constants = moduli.reshape(3, 1, 1)
    stiff_a = constants[0]
    stiff_b = constants[1]
    shear = constants[2]
    strain = eigenstrain
    trace = strain[:, 0:1] + strain[:, 1:2] + strain[:, 2:3]
    stress = jnp.concatenate(
        [
            moduli[1:2] * trace + (moduli[0:1] - moduli[1:2]) * strain[:, 0:3],
            2.0 * moduli[2:3] * strain[:, 3:6],
        ],
        axis=1,
    )
    voigt = [[0, 5, 4], [5, 1, 3], [4, 3, 2]]
    energy = sum(
        (
            stress[:, None, voigt[first][second]] * strain[None, :, voigt[first][second]]
            for first in range(3)
            for second in range(3)
        )
    )
    width = kx_wave.shape[-1]
    constants = jnp.broadcast_to(moduli[:, None], (3, width))
    stress_b = jnp.broadcast_to(stress[:, :, None], (3, 6, width))
    energy = jnp.broadcast_to(energy[:, :, None], (3, 3, width))
    constants, stress_b, energy = lax.optimization_barrier((constants, stress_b, energy))
    stiff_a = constants[0]
    stiff_b = constants[1]
    shear = constants[2]
    square = kx_wave * kx_wave + ky_wave * ky_wave + kz_wave * kz_wave
    inside = square > 0.0
    inverse = lax.rsqrt(jnp.where(inside, square, 1.0))
    normal = [kx_wave * inverse, ky_wave * inverse, kz_wave * inverse]
    g_diag = [shear + (stiff_a - shear) * normal[axis_id] * normal[axis_id] for axis_id in range(3)]
    cross_coef = stiff_b + shear
    g_zero_one = cross_coef * normal[0] * normal[1]
    g_zero_two = cross_coef * normal[0] * normal[2]
    g_one_two = cross_coef * normal[1] * normal[2]
    cof_zz = g_diag[1] * g_diag[2] - g_one_two * g_one_two
    cof_zo = g_zero_two * g_one_two - g_zero_one * g_diag[2]
    cof_zt = g_zero_one * g_one_two - g_zero_two * g_diag[1]
    cof_oo = g_diag[0] * g_diag[2] - g_zero_two * g_zero_two
    cof_ot = g_zero_one * g_zero_two - g_diag[0] * g_one_two
    cof_tt = g_diag[0] * g_diag[1] - g_zero_one * g_zero_one
    determinant = g_diag[0] * cof_zz + g_zero_one * cof_zo + g_zero_two * cof_zt
    recip = 1.0 / determinant
    omega = [
        [cof_zz * recip, cof_zo * recip, cof_zt * recip],
        [cof_zo * recip, cof_oo * recip, cof_ot * recip],
        [cof_zt * recip, cof_ot * recip, cof_tt * recip],
    ]
    traction = []
    for variant in range(3):
        traction.append(
            [
                sum((stress_b[variant, voigt[first][second]] * normal[second] for second in range(3)))
                for first in range(3)
            ]
        )
    response = []
    for variant in range(3):
        response.append(
            [
                sum((omega[first][second] * traction[variant][second] for second in range(3)))
                for first in range(3)
            ]
        )
    kernel = []
    for source in range(3):
        kernel_row = []
        for target in range(3):
            coupling = sum(
                (traction[source][first] * response[target][first] for first in range(3))
            )
            kernel_row.append(jnp.where(inside, energy[source, target] - coupling, 0.0))
        kernel.append(kernel_row)
    return kernel


def cos_sin(numer, length):
    angle = (2.0 * math.pi / length) * (numer % length).astype(jnp.float32)
    return (jnp.cos(angle), jnp.sin(angle))


def np_cos_sin(numer, length):
    angle = (2.0 * np.pi / length) * (numer % length).astype(np.float64)
    return (np.cos(angle).astype(np.float32), np.sin(angle).astype(np.float32))


def stacked_table(length):
    index = np.arange(length)
    cosine, sine = np_cos_sin(np.outer(index, index), length)
    return np.concatenate([cosine, sine], axis=0)


def block_dft8():
    size = 192
    rows_idx = np.arange(size)[:, None]
    cols_idx = np.arange(size)[None, :]
    same = (rows_idx // 32 == cols_idx // 32) & (rows_idx % 4 == cols_idx % 4)
    cosine, sine = np_cos_sin(((rows_idx // 4) % 8) * ((cols_idx // 4) % 8), 8)
    cosine = np.where(same, cosine, 0.0).astype(np.float32)
    sine = np.where(same, sine, 0.0).astype(np.float32)
    top = np.concatenate([cosine, -sine], axis=1)
    bottom = np.concatenate([sine, cosine], axis=1)
    return np.concatenate([top, bottom], axis=0)


def z_twiddle_table():
    rows_idx = np.arange(128)[:, None]
    cols_idx = np.arange(192)[None, :]
    return np.stack(np_cos_sin(rows_idx * ((cols_idx // 4) % 8), 1024))


def y_twiddle_table():
    return np.stack(np_cos_sin(np.arange(4)[:, None] * np.arange(128)[None, :], 512))


def matmul(spec, left, right):
    return jnp.einsum(spec, left, right, precision=highest)


def combine_rows(product, sign):
    c_re = product[:128, :192]
    c_im = product[:128, 192:]
    s_re = product[128:, :192]
    s_im = product[128:, 192:]
    if sign < 0:
        return (c_re + s_im, c_im - s_re)
    return (c_re - s_im, c_im + s_re)


def twiddle(values, factor_cos, factor_sin):
    real_part = values[0] * factor_cos - values[1] * factor_sin
    imag_part = values[1] * factor_cos + values[0] * factor_sin
    return jnp.stack([real_part, imag_part])


def rotate_neg(values):
    return jnp.stack([values[1], -values[0]])


def rotate_pos(values):
    return jnp.stack([-values[1], values[0]])


def times_i(re, im, sign):
    return (-sign * im, sign * re)


def dft4(parts, sign):
    (r0, i0), (r1, i1), (r2, i2), (r3, i3) = parts
    ar, ai = r0 + r2, i0 + i2
    br, bi = r0 - r2, i0 - i2
    cr, ci = r1 + r3, i1 + i3
    dr, di = times_i(r1 - r3, i1 - i3, sign)
    return [(ar + cr, ai + ci), (br + dr, bi + di), (ar - cr, ai - ci), (br - dr, bi - di)]


def dft4_across(gathered, index, sign):
    (r0, i0), (r1, i1), (r2, i2), (r3, i3) = [(gathered[g, 0], gathered[g, 1]) for g in range(4)]
    ar, ai = r0 + r2, i0 + i2
    br, bi = r0 - r2, i0 - i2
    cr, ci = r1 + r3, i1 + i3
    dr, di = times_i(r1 - r3, i1 - i3, sign)
    choices = [(ar + cr, ai + ci), (br + dr, bi + di), (ar - cr, ai - ci), (br - dr, bi - di)]
    real_part = choices[3][0]
    imag_part = choices[3][1]
    for position in (2, 1, 0):
        real_part = jnp.where(index == position, choices[position][0], real_part)
        imag_part = jnp.where(index == position, choices[position][1], imag_part)
    return jnp.stack([real_part, imag_part])


def y_forward(spectral):
    parts = [(spectral[0, ..., 128 * a:128 * a + 128], spectral[1, ..., 128 * a:128 * a + 128]) for a in range(4)]
    mixed = dft4(parts, -1)
    table = y_twiddle_table()
    out = []
    for k1 in range(4):
        tw_cos, tw_sin = table[0, k1], table[1, k1]
        re, im = mixed[k1]
        out.append(jnp.stack([re * tw_cos + im * tw_sin, im * tw_cos - re * tw_sin]))
    stacked = jnp.stack(out, axis=-2).reshape(384, 128)
    product = matmul("kb,rb->kr", stacked_table(128), stacked)
    re, im = combine_rows(product, -1)
    return jnp.concatenate([re, im], axis=1)


def y_inverse(returned):
    product = matmul("kr,bk->rb", returned, stacked_table(128))
    c_re = product[:192, :128]
    s_re = product[:192, 128:]
    c_im = product[192:, :128]
    s_im = product[192:, 128:]
    re = (c_re - s_im).reshape(3, 2, 8, 4, 128)
    im = (c_im + s_re).reshape(3, 2, 8, 4, 128)
    table = y_twiddle_table()
    parts = []
    for k1 in range(4):
        tw_cos, tw_sin = table[0, k1], table[1, k1]
        r = re[..., k1, :]
        i = im[..., k1, :]
        parts.append((r * tw_cos - i * tw_sin, i * tw_cos + r * tw_sin))
    mixed = dft4(parts, 1)
    real_part = jnp.concatenate([m[0] for m in mixed], axis=-1)
    imag_part = jnp.concatenate([m[1] for m in mixed], axis=-1)
    return jnp.stack([real_part, imag_part])


def z_twiddle(re, im, sign):
    table = z_twiddle_table()
    tw_cos = table[0]
    tw_sin = sign * table[1]
    return jnp.concatenate([re * tw_cos - im * tw_sin, im * tw_cos + re * tw_sin], axis=1)


def shards(fields, eigenstrain, moduli):
    gy_count = lax.axis_size("gy")
    gy_index = lax.axis_index("gy")
    gz_index = lax.axis_index("gz")
    y_local = fields.shape[4]
    positions = lax.broadcasted_iota(jnp.int32, (y_local,), 0)
    spectral = dft4_across(lax.all_gather(fields, "gy", axis=0), gy_index, -1)
    residue = gy_index
    angle = 2.0 * math.pi / NY * (positions * residue % NY).astype(jnp.float32)
    phase_cos = jnp.cos(angle)
    phase_sin = jnp.sin(angle)
    spectral = twiddle(spectral, phase_cos, -phase_sin)
    slabs = y_forward(spectral)
    pencils = lax.all_to_all(slabs, "gz", split_axis=0, concat_axis=0, tiled=True)
    table = stacked_table(128)
    re, im = combine_rows(matmul("kg,gc->kc", table, pencils), -1)
    spectrum = jnp.dot(z_twiddle(re, im, -1), block_dft8(), precision=highest)
    rows_idx = lax.broadcasted_iota(jnp.int32, (128, 64), 0)
    cols_idx = lax.broadcasted_iota(jnp.int32, (128, 64), 1)
    plane = cols_idx // 32
    kz_index = rows_idx + 128 * ((cols_idx // 4) % 8)
    ky_index = residue + gy_count * (cols_idx % 4 + 4 * gz_index)
    kx_wave = plane.astype(jnp.float32) / NX
    ky_wave = signed_wave(ky_index, NY)
    kz_wave = signed_wave(kz_index, NZ)
    kernel = kernel_rows(kx_wave, ky_wave, kz_wave, eigenstrain, moduli)
    scale = 1.0 / (NY * NZ)
    spec = spectrum.reshape(128, 2, 3, 64)
    forced = jnp.stack(
        [
            jnp.stack(
                [
                    sum((kernel[source][target] * spec[:, part, target] for target in range(3))) * scale
                    for source in range(3)
                ],
                axis=1,
            )
            for part in range(2)
        ],
        axis=1,
    ).reshape(128, 384)
    back = matmul("kr,sr->ks", forced, block_dft8())
    back = z_twiddle(back[:, :192], back[:, 192:], 1)
    re, im = combine_rows(matmul("kg,gc->kc", table, back), 1)
    back = jnp.concatenate([re, im], axis=1)
    returned = lax.all_to_all(back, "gz", split_axis=0, concat_axis=0, tiled=True)
    spatial = y_inverse(returned)
    spatial = twiddle(spatial, phase_cos, phase_sin)
    result = dft4_across(lax.all_gather(spatial, "gy", axis=0), gy_index, 1)
    return result


def solution(mesh):
    in_specs = (P(None, None, None, "gz", "gy"), P(), P())
    out_specs = P(None, None, None, "gz", "gy")
    return jax.shard_map(shards, mesh=mesh, in_specs=in_specs, out_specs=out_specs, check_vma=False)
```

```python
import math

import numpy as np

import jax
import jax.numpy as jnp
from jax import lax
from jax.sharding import PartitionSpec as P

NX = 2048
NY = 2048
NZ = 1024


highest = lax.Precision.HIGH


def partner_2(value, axis, stride):
    mask = 2**stride
    pairs = [(source, source ^ mask) for source in range(lax.axis_size(axis))]
    return lax.ppermute(value, axis, pairs)


def signed_wave(index, length):
    return jnp.where(index < length // 2, index, index - length).astype(jnp.float32) / length


def kernel_rows(kx_wave, ky_wave, kz_wave, eigenstrain, moduli):
    constants = moduli.reshape(3, 1, 1)
    stiff_a = constants[0]
    stiff_b = constants[1]
    shear = constants[2]
    strain = eigenstrain
    trace = strain[:, 0:1] + strain[:, 1:2] + strain[:, 2:3]
    stress = jnp.concatenate(
        [
            moduli[1:2] * trace + (moduli[0:1] - moduli[1:2]) * strain[:, 0:3],
            2.0 * moduli[2:3] * strain[:, 3:6],
        ],
        axis=1,
    )
    voigt = [[0, 5, 4], [5, 1, 3], [4, 3, 2]]
    energy = sum(
        (
            stress[:, None, voigt[first][second]] * strain[None, :, voigt[first][second]]
            for first in range(3)
            for second in range(3)
        )
    )
    width = kx_wave.shape[-1]
    constants = jnp.broadcast_to(moduli[:, None], (3, width))
    stress_b = jnp.broadcast_to(stress[:, :, None], (3, 6, width))
    energy = jnp.broadcast_to(energy[:, :, None], (3, 3, width))
    constants, stress_b, energy = lax.optimization_barrier((constants, stress_b, energy))
    stiff_a = constants[0]
    stiff_b = constants[1]
    shear = constants[2]
    square = kx_wave * kx_wave + ky_wave * ky_wave + kz_wave * kz_wave
    inside = square > 0.0
    inverse = lax.rsqrt(jnp.where(inside, square, 1.0))
    normal = [kx_wave * inverse, ky_wave * inverse, kz_wave * inverse]
    g_diag = [shear + (stiff_a - shear) * normal[axis_id] * normal[axis_id] for axis_id in range(3)]
    cross_coef = stiff_b + shear
    g_zero_one = cross_coef * normal[0] * normal[1]
    g_zero_two = cross_coef * normal[0] * normal[2]
    g_one_two = cross_coef * normal[1] * normal[2]
    cof_zz = g_diag[1] * g_diag[2] - g_one_two * g_one_two
    cof_zo = g_zero_two * g_one_two - g_zero_one * g_diag[2]
    cof_zt = g_zero_one * g_one_two - g_zero_two * g_diag[1]
    cof_oo = g_diag[0] * g_diag[2] - g_zero_two * g_zero_two
    cof_ot = g_zero_one * g_zero_two - g_diag[0] * g_one_two
    cof_tt = g_diag[0] * g_diag[1] - g_zero_one * g_zero_one
    determinant = g_diag[0] * cof_zz + g_zero_one * cof_zo + g_zero_two * cof_zt
    recip = 1.0 / determinant
    omega = [
        [cof_zz * recip, cof_zo * recip, cof_zt * recip],
        [cof_zo * recip, cof_oo * recip, cof_ot * recip],
        [cof_zt * recip, cof_ot * recip, cof_tt * recip],
    ]
    traction = []
    for variant in range(3):
        traction.append(
            [
                sum((stress_b[variant, voigt[first][second]] * normal[second] for second in range(3)))
                for first in range(3)
            ]
        )
    response = []
    for variant in range(3):
        response.append(
            [
                sum((omega[first][second] * traction[variant][second] for second in range(3)))
                for first in range(3)
            ]
        )
    kernel = []
    for source in range(3):
        kernel_row = []
        for target in range(3):
            coupling = sum(
                (traction[source][first] * response[target][first] for first in range(3))
            )
            kernel_row.append(jnp.where(inside, energy[source, target] - coupling, 0.0))
        kernel.append(kernel_row)
    return kernel


def cos_sin(numer, length):
    angle = (2.0 * math.pi / length) * (numer % length).astype(jnp.float32)
    return (jnp.cos(angle), jnp.sin(angle))


def np_cos_sin(numer, length):
    angle = (2.0 * np.pi / length) * (numer % length).astype(np.float64)
    return (np.cos(angle).astype(np.float32), np.sin(angle).astype(np.float32))


def stacked_table(length):
    index = np.arange(length)
    cosine, sine = np_cos_sin(np.outer(index, index), length)
    return np.concatenate([cosine, sine], axis=0)


def block_dft8():
    size = 192
    rows_idx = lax.broadcasted_iota(jnp.int32, (size, size), 0)
    cols_idx = lax.broadcasted_iota(jnp.int32, (size, size), 1)
    same = (rows_idx // 32 == cols_idx // 32) & (rows_idx % 4 == cols_idx % 4)
    cosine, sine = cos_sin(((rows_idx // 4) % 8) * ((cols_idx // 4) % 8), 8)
    cosine = jnp.where(same, cosine, 0.0)
    sine = jnp.where(same, sine, 0.0)
    top = jnp.concatenate([cosine, -sine], axis=1)
    bottom = jnp.concatenate([sine, cosine], axis=1)
    return jnp.concatenate([top, bottom], axis=0)


def z_twiddle_table():
    rows_idx = lax.broadcasted_iota(jnp.int32, (128, 192), 0)
    cols_idx = lax.broadcasted_iota(jnp.int32, (128, 192), 1)
    return jnp.stack(cos_sin(rows_idx * ((cols_idx // 4) % 8), 1024))


def y_twiddle_table():
    return np.stack(np_cos_sin(np.arange(4)[:, None] * np.arange(128)[None, :], 512))


def matmul(spec, left, right):
    return jnp.einsum(spec, left, right, precision=highest)


def combine_rows(product, sign):
    c_re = product[:128, :192]
    c_im = product[:128, 192:]
    s_re = product[128:, :192]
    s_im = product[128:, 192:]
    if sign < 0:
        return (c_re + s_im, c_im - s_re)
    return (c_re - s_im, c_im + s_re)


def twiddle(values, factor_cos, factor_sin):
    real_part = values[0] * factor_cos - values[1] * factor_sin
    imag_part = values[1] * factor_cos + values[0] * factor_sin
    return jnp.stack([real_part, imag_part])


def rotate_neg(values):
    return jnp.stack([values[1], -values[0]])


def rotate_pos(values):
    return jnp.stack([-values[1], values[0]])


def times_i(re, im, sign):
    return (-sign * im, sign * re)


def dft4(parts, sign):
    (r0, i0), (r1, i1), (r2, i2), (r3, i3) = parts
    ar, ai = r0 + r2, i0 + i2
    br, bi = r0 - r2, i0 - i2
    cr, ci = r1 + r3, i1 + i3
    dr, di = times_i(r1 - r3, i1 - i3, sign)
    return [(ar + cr, ai + ci), (br + dr, bi + di), (ar - cr, ai - ci), (br - dr, bi - di)]


def dft4_across(gathered, index, sign):
    (r0, i0), (r1, i1), (r2, i2), (r3, i3) = [(gathered[g, 0], gathered[g, 1]) for g in range(4)]
    ar, ai = r0 + r2, i0 + i2
    br, bi = r0 - r2, i0 - i2
    cr, ci = r1 + r3, i1 + i3
    dr, di = times_i(r1 - r3, i1 - i3, sign)
    choices = [(ar + cr, ai + ci), (br + dr, bi + di), (ar - cr, ai - ci), (br - dr, bi - di)]
    real_part = choices[3][0]
    imag_part = choices[3][1]
    for position in (2, 1, 0):
        real_part = jnp.where(index == position, choices[position][0], real_part)
        imag_part = jnp.where(index == position, choices[position][1], imag_part)
    return jnp.stack([real_part, imag_part])


def y_forward(spectral):
    parts = [(spectral[0, ..., 128 * a:128 * a + 128], spectral[1, ..., 128 * a:128 * a + 128]) for a in range(4)]
    mixed = dft4(parts, -1)
    table = y_twiddle_table()
    out = []
    for k1 in range(4):
        tw_cos, tw_sin = table[0, k1], table[1, k1]
        re, im = mixed[k1]
        out.append(jnp.stack([re * tw_cos + im * tw_sin, im * tw_cos - re * tw_sin]))
    stacked = jnp.stack(out, axis=-2).reshape(384, 128)
    product = matmul("kb,rb->kr", stacked_table(128), stacked)
    re, im = combine_rows(product, -1)
    return jnp.concatenate([re, im], axis=1)


def y_inverse(returned):
    product = matmul("kr,bk->rb", returned, stacked_table(128))
    c_re = product[:192, :128]
    s_re = product[:192, 128:]
    c_im = product[192:, :128]
    s_im = product[192:, 128:]
    re = (c_re - s_im).reshape(3, 2, 8, 4, 128)
    im = (c_im + s_re).reshape(3, 2, 8, 4, 128)
    table = y_twiddle_table()
    parts = []
    for k1 in range(4):
        tw_cos, tw_sin = table[0, k1], table[1, k1]
        r = re[..., k1, :]
        i = im[..., k1, :]
        parts.append((r * tw_cos - i * tw_sin, i * tw_cos + r * tw_sin))
    mixed = dft4(parts, 1)
    real_part = jnp.concatenate([m[0] for m in mixed], axis=-1)
    imag_part = jnp.concatenate([m[1] for m in mixed], axis=-1)
    return jnp.stack([real_part, imag_part])


def z_twiddle(re, im, sign):
    table = z_twiddle_table()
    tw_cos = table[0]
    tw_sin = sign * table[1]
    return jnp.concatenate([re * tw_cos - im * tw_sin, im * tw_cos + re * tw_sin], axis=1)


def shards(fields, eigenstrain, moduli):
    gy_count = lax.axis_size("gy")
    gy_index = lax.axis_index("gy")
    gz_index = lax.axis_index("gz")
    y_local = fields.shape[4]
    positions = lax.broadcasted_iota(jnp.int32, (y_local,), 0)
    spectral = dft4_across(lax.all_gather(fields, "gy", axis=0), gy_index, -1)
    residue = gy_index
    angle = 2.0 * math.pi / NY * (positions * residue % NY).astype(jnp.float32)
    phase_cos = jnp.cos(angle)
    phase_sin = jnp.sin(angle)
    spectral = twiddle(spectral, phase_cos, -phase_sin)
    slabs = y_forward(spectral)
    pencils = lax.all_to_all(slabs, "gz", split_axis=0, concat_axis=0, tiled=True)
    table = stacked_table(128)
    re, im = combine_rows(matmul("kg,gc->kc", table, pencils), -1)
    spectrum = jnp.dot(z_twiddle(re, im, -1), block_dft8(), precision=highest)
    rows_idx = lax.broadcasted_iota(jnp.int32, (128, 64), 0)
    cols_idx = lax.broadcasted_iota(jnp.int32, (128, 64), 1)
    plane = cols_idx // 32
    kz_index = rows_idx + 128 * ((cols_idx // 4) % 8)
    ky_index = residue + gy_count * (cols_idx % 4 + 4 * gz_index)
    kx_wave = plane.astype(jnp.float32) / NX
    ky_wave = signed_wave(ky_index, NY)
    kz_wave = signed_wave(kz_index, NZ)
    kernel = kernel_rows(kx_wave, ky_wave, kz_wave, eigenstrain, moduli)
    scale = 1.0 / (NY * NZ)
    spec = spectrum.reshape(128, 2, 3, 64)
    forced = jnp.stack(
        [
            jnp.stack(
                [
                    sum((kernel[source][target] * spec[:, part, target] for target in range(3))) * scale
                    for source in range(3)
                ],
                axis=1,
            )
            for part in range(2)
        ],
        axis=1,
    ).reshape(128, 384)
    back = matmul("kr,sr->ks", forced, block_dft8())
    back = z_twiddle(back[:, :192], back[:, 192:], 1)
    re, im = combine_rows(matmul("kg,gc->kc", table, back), 1)
    back = jnp.concatenate([re, im], axis=1)
    returned = lax.all_to_all(back, "gz", split_axis=0, concat_axis=0, tiled=True)
    spatial = y_inverse(returned)
    spatial = twiddle(spatial, phase_cos, phase_sin)
    result = dft4_across(lax.all_gather(spatial, "gy", axis=0), gy_index, 1)
    return result


def solution(mesh):
    in_specs = (P(None, None, None, "gz", "gy"), P(), P())
    out_specs = P(None, None, None, "gz", "gy")
    return jax.shard_map(shards, mesh=mesh, in_specs=in_specs, out_specs=out_specs, check_vma=False)
```

```python
import math

import numpy as np

import jax
import jax.numpy as jnp
from jax import lax
from jax.sharding import PartitionSpec as P

NX = 2048
NY = 2048
NZ = 1024


highest = lax.Precision.HIGH


def partner_2(value, axis, stride):
    mask = 2**stride
    pairs = [(source, source ^ mask) for source in range(lax.axis_size(axis))]
    return lax.ppermute(value, axis, pairs)


def signed_wave(index, length):
    return jnp.where(index < length // 2, index, index - length).astype(jnp.float32) / length


def kernel_rows(kx_wave, ky_wave, kz_wave, eigenstrain, moduli):
    constants = moduli.reshape(3, 1, 1)
    stiff_a = constants[0]
    stiff_b = constants[1]
    shear = constants[2]
    strain = eigenstrain
    trace = strain[:, 0:1] + strain[:, 1:2] + strain[:, 2:3]
    stress = jnp.concatenate(
        [
            moduli[1:2] * trace + (moduli[0:1] - moduli[1:2]) * strain[:, 0:3],
            2.0 * moduli[2:3] * strain[:, 3:6],
        ],
        axis=1,
    )
    voigt = [[0, 5, 4], [5, 1, 3], [4, 3, 2]]
    energy = sum(
        (
            stress[:, None, voigt[first][second]] * strain[None, :, voigt[first][second]]
            for first in range(3)
            for second in range(3)
        )
    )
    width = kx_wave.shape[-1]
    constants = jnp.broadcast_to(moduli[:, None], (3, width))
    stress_b = jnp.broadcast_to(stress[:, :, None], (3, 6, width))
    energy = jnp.broadcast_to(energy[:, :, None], (3, 3, width))
    constants, stress_b, energy = lax.optimization_barrier((constants, stress_b, energy))
    stiff_a = constants[0]
    stiff_b = constants[1]
    shear = constants[2]
    square = kx_wave * kx_wave + ky_wave * ky_wave + kz_wave * kz_wave
    inside = square > 0.0
    inverse = lax.rsqrt(jnp.where(inside, square, 1.0))
    normal = [kx_wave * inverse, ky_wave * inverse, kz_wave * inverse]
    g_diag = [shear + (stiff_a - shear) * normal[axis_id] * normal[axis_id] for axis_id in range(3)]
    cross_coef = stiff_b + shear
    g_zero_one = cross_coef * normal[0] * normal[1]
    g_zero_two = cross_coef * normal[0] * normal[2]
    g_one_two = cross_coef * normal[1] * normal[2]
    cof_zz = g_diag[1] * g_diag[2] - g_one_two * g_one_two
    cof_zo = g_zero_two * g_one_two - g_zero_one * g_diag[2]
    cof_zt = g_zero_one * g_one_two - g_zero_two * g_diag[1]
    cof_oo = g_diag[0] * g_diag[2] - g_zero_two * g_zero_two
    cof_ot = g_zero_one * g_zero_two - g_diag[0] * g_one_two
    cof_tt = g_diag[0] * g_diag[1] - g_zero_one * g_zero_one
    determinant = g_diag[0] * cof_zz + g_zero_one * cof_zo + g_zero_two * cof_zt
    recip = 1.0 / determinant
    omega = [
        [cof_zz * recip, cof_zo * recip, cof_zt * recip],
        [cof_zo * recip, cof_oo * recip, cof_ot * recip],
        [cof_zt * recip, cof_ot * recip, cof_tt * recip],
    ]
    traction = []
    for variant in range(3):
        traction.append(
            [
                sum((stress_b[variant, voigt[first][second]] * normal[second] for second in range(3)))
                for first in range(3)
            ]
        )
    response = []
    for variant in range(3):
        response.append(
            [
                sum((omega[first][second] * traction[variant][second] for second in range(3)))
                for first in range(3)
            ]
        )
    kernel = []
    for source in range(3):
        kernel_row = []
        for target in range(3):
            coupling = sum(
                (traction[source][first] * response[target][first] for first in range(3))
            )
            kernel_row.append(jnp.where(inside, energy[source, target] - coupling, 0.0))
        kernel.append(kernel_row)
    return kernel


def cos_sin(numer, length):
    angle = (2.0 * math.pi / length) * (numer % length).astype(jnp.float32)
    return (jnp.cos(angle), jnp.sin(angle))


def np_cos_sin(numer, length):
    angle = (2.0 * np.pi / length) * (numer % length).astype(np.float64)
    return (np.cos(angle).astype(np.float32), np.sin(angle).astype(np.float32))


def stacked_table(length):
    index = np.arange(length)
    cosine, sine = np_cos_sin(np.outer(index, index), length)
    return np.concatenate([cosine, sine], axis=0)


def block_dft8():
    size = 192
    rows_idx = lax.broadcasted_iota(jnp.int32, (size, size), 0)
    cols_idx = lax.broadcasted_iota(jnp.int32, (size, size), 1)
    same = (rows_idx // 32 == cols_idx // 32) & (rows_idx % 4 == cols_idx % 4)
    cosine, sine = cos_sin(((rows_idx // 4) % 8) * ((cols_idx // 4) % 8), 8)
    cosine = jnp.where(same, cosine, 0.0)
    sine = jnp.where(same, sine, 0.0)
    top = jnp.concatenate([cosine, -sine], axis=1)
    bottom = jnp.concatenate([sine, cosine], axis=1)
    return jnp.concatenate([top, bottom], axis=0)


def z_twiddle_table():
    rows_idx = lax.broadcasted_iota(jnp.int32, (128, 192), 0)
    cols_idx = lax.broadcasted_iota(jnp.int32, (128, 192), 1)
    return jnp.stack(cos_sin(rows_idx * ((cols_idx // 4) % 8), 1024))


def matmul(spec, left, right):
    return jnp.einsum(spec, left, right, precision=highest)


def combine_rows(product, sign):
    c_re = product[:128, :192]
    c_im = product[:128, 192:]
    s_re = product[128:, :192]
    s_im = product[128:, 192:]
    if sign < 0:
        return (c_re + s_im, c_im - s_re)
    return (c_re - s_im, c_im + s_re)


def twiddle(values, factor_cos, factor_sin):
    real_part = values[0] * factor_cos - values[1] * factor_sin
    imag_part = values[1] * factor_cos + values[0] * factor_sin
    return jnp.stack([real_part, imag_part])


def rotate_neg(values):
    return jnp.stack([values[1], -values[0]])


def rotate_pos(values):
    return jnp.stack([-values[1], values[0]])


def times_i(re, im, sign):
    return (-sign * im, sign * re)


def dft4(parts, sign):
    (r0, i0), (r1, i1), (r2, i2), (r3, i3) = parts
    ar, ai = r0 + r2, i0 + i2
    br, bi = r0 - r2, i0 - i2
    cr, ci = r1 + r3, i1 + i3
    dr, di = times_i(r1 - r3, i1 - i3, sign)
    return [(ar + cr, ai + ci), (br + dr, bi + di), (ar - cr, ai - ci), (br - dr, bi - di)]


def dft4_across(gathered, index, sign):
    (r0, i0), (r1, i1), (r2, i2), (r3, i3) = [(gathered[g, 0], gathered[g, 1]) for g in range(4)]
    ar, ai = r0 + r2, i0 + i2
    br, bi = r0 - r2, i0 - i2
    cr, ci = r1 + r3, i1 + i3
    dr, di = times_i(r1 - r3, i1 - i3, sign)
    choices = [(ar + cr, ai + ci), (br + dr, bi + di), (ar - cr, ai - ci), (br - dr, bi - di)]
    real_part = choices[3][0]
    imag_part = choices[3][1]
    for position in (2, 1, 0):
        real_part = jnp.where(index == position, choices[position][0], real_part)
        imag_part = jnp.where(index == position, choices[position][1], imag_part)
    return jnp.stack([real_part, imag_part])


def y_forward(spectral):
    parts = [(spectral[0, ..., 128 * a:128 * a + 128], spectral[1, ..., 128 * a:128 * a + 128]) for a in range(4)]
    mixed = dft4(parts, -1)
    lanes = lax.broadcasted_iota(jnp.int32, (128,), 0)
    out = []
    for k1 in range(4):
        tw_cos, tw_sin = cos_sin(lanes * k1, 512)
        re, im = mixed[k1]
        out.append(jnp.stack([re * tw_cos + im * tw_sin, im * tw_cos - re * tw_sin]))
    stacked = jnp.stack(out, axis=-2).reshape(384, 128)
    product = matmul("kb,rb->kr", stacked_table(128), stacked)
    re, im = combine_rows(product, -1)
    return jnp.concatenate([re, im], axis=1)


def y_inverse(returned):
    product = matmul("kr,bk->rb", returned, stacked_table(128))
    c_re = product[:192, :128]
    s_re = product[:192, 128:]
    c_im = product[192:, :128]
    s_im = product[192:, 128:]
    re = (c_re - s_im).reshape(3, 2, 8, 4, 128)
    im = (c_im + s_re).reshape(3, 2, 8, 4, 128)
    lanes = lax.broadcasted_iota(jnp.int32, (128,), 0)
    parts = []
    for k1 in range(4):
        tw_cos, tw_sin = cos_sin(lanes * k1, 512)
        r = re[..., k1, :]
        i = im[..., k1, :]
        parts.append((r * tw_cos - i * tw_sin, i * tw_cos + r * tw_sin))
    mixed = dft4(parts, 1)
    real_part = jnp.concatenate([m[0] for m in mixed], axis=-1)
    imag_part = jnp.concatenate([m[1] for m in mixed], axis=-1)
    return jnp.stack([real_part, imag_part])


def z_twiddle(re, im, sign):
    table = z_twiddle_table()
    tw_cos = table[0]
    tw_sin = sign * table[1]
    return jnp.concatenate([re * tw_cos - im * tw_sin, im * tw_cos + re * tw_sin], axis=1)


def shards(fields, eigenstrain, moduli):
    gy_count = lax.axis_size("gy")
    gy_index = lax.axis_index("gy")
    gz_index = lax.axis_index("gz")
    y_local = fields.shape[4]
    positions = lax.broadcasted_iota(jnp.int32, (y_local,), 0)
    spectral = dft4_across(lax.all_gather(fields, "gy", axis=0), gy_index, -1)
    residue = gy_index
    angle = 2.0 * math.pi / NY * (positions * residue % NY).astype(jnp.float32)
    phase_cos = jnp.cos(angle)
    phase_sin = jnp.sin(angle)
    spectral = twiddle(spectral, phase_cos, -phase_sin)
    slabs = y_forward(spectral)
    pencils = lax.all_to_all(slabs, "gz", split_axis=0, concat_axis=0, tiled=True)
    table = stacked_table(128)
    re, im = combine_rows(matmul("kg,gc->kc", table, pencils), -1)
    spectrum = jnp.dot(z_twiddle(re, im, -1), block_dft8(), precision=highest)
    rows_idx = lax.broadcasted_iota(jnp.int32, (128, 64), 0)
    cols_idx = lax.broadcasted_iota(jnp.int32, (128, 64), 1)
    plane = cols_idx // 32
    kz_index = rows_idx + 128 * ((cols_idx // 4) % 8)
    ky_index = residue + gy_count * (cols_idx % 4 + 4 * gz_index)
    kx_wave = plane.astype(jnp.float32) / NX
    ky_wave = signed_wave(ky_index, NY)
    kz_wave = signed_wave(kz_index, NZ)
    kernel = kernel_rows(kx_wave, ky_wave, kz_wave, eigenstrain, moduli)
    scale = 1.0 / (NY * NZ)
    spec = spectrum.reshape(128, 2, 3, 64)
    forced = jnp.stack(
        [
            jnp.stack(
                [
                    sum((kernel[source][target] * spec[:, part, target] for target in range(3))) * scale
                    for source in range(3)
                ],
                axis=1,
            )
            for part in range(2)
        ],
        axis=1,
    ).reshape(128, 384)
    back = matmul("kr,sr->ks", forced, block_dft8())
    back = z_twiddle(back[:, :192], back[:, 192:], 1)
    re, im = combine_rows(matmul("kg,gc->kc", table, back), 1)
    back = jnp.concatenate([re, im], axis=1)
    returned = lax.all_to_all(back, "gz", split_axis=0, concat_axis=0, tiled=True)
    spatial = y_inverse(returned)
    spatial = twiddle(spatial, phase_cos, phase_sin)
    result = dft4_across(lax.all_gather(spatial, "gy", axis=0), gy_index, 1)
    return result


def solution(mesh):
    in_specs = (P(None, None, None, "gz", "gy"), P(), P())
    out_specs = P(None, None, None, "gz", "gy")
    return jax.shard_map(shards, mesh=mesh, in_specs=in_specs, out_specs=out_specs, check_vma=False)
```

```python
import math

import numpy as np

import jax
import jax.numpy as jnp
from jax import lax
from jax.sharding import PartitionSpec as P

NX = 2048
NY = 2048
NZ = 1024


highest = lax.Precision.HIGHEST


def partner_2(value, axis, stride):
    mask = 2**stride
    pairs = [(source, source ^ mask) for source in range(lax.axis_size(axis))]
    return lax.ppermute(value, axis, pairs)


def signed_wave(index, length):
    return jnp.where(index < length // 2, index, index - length).astype(jnp.float32) / length


def kernel_rows(kx_wave, ky_wave, kz_wave, eigenstrain, moduli):
    constants = moduli.reshape(3, 1, 1)
    stiff_a = constants[0]
    stiff_b = constants[1]
    shear = constants[2]
    strain = eigenstrain
    trace = strain[:, 0:1] + strain[:, 1:2] + strain[:, 2:3]
    stress = jnp.concatenate(
        [
            moduli[1:2] * trace + (moduli[0:1] - moduli[1:2]) * strain[:, 0:3],
            2.0 * moduli[2:3] * strain[:, 3:6],
        ],
        axis=1,
    )
    voigt = [[0, 5, 4], [5, 1, 3], [4, 3, 2]]
    energy = sum(
        (
            stress[:, None, voigt[first][second]] * strain[None, :, voigt[first][second]]
            for first in range(3)
            for second in range(3)
        )
    )
    width = kx_wave.shape[-1]
    constants = jnp.broadcast_to(moduli[:, None], (3, width))
    stress_b = jnp.broadcast_to(stress[:, :, None], (3, 6, width))
    energy = jnp.broadcast_to(energy[:, :, None], (3, 3, width))
    constants, stress_b, energy = lax.optimization_barrier((constants, stress_b, energy))
    stiff_a = constants[0]
    stiff_b = constants[1]
    shear = constants[2]
    square = kx_wave * kx_wave + ky_wave * ky_wave + kz_wave * kz_wave
    inside = square > 0.0
    inverse = lax.rsqrt(jnp.where(inside, square, 1.0))
    normal = [kx_wave * inverse, ky_wave * inverse, kz_wave * inverse]
    g_diag = [shear + (stiff_a - shear) * normal[axis_id] * normal[axis_id] for axis_id in range(3)]
    cross_coef = stiff_b + shear
    g_zero_one = cross_coef * normal[0] * normal[1]
    g_zero_two = cross_coef * normal[0] * normal[2]
    g_one_two = cross_coef * normal[1] * normal[2]
    cof_zz = g_diag[1] * g_diag[2] - g_one_two * g_one_two
    cof_zo = g_zero_two * g_one_two - g_zero_one * g_diag[2]
    cof_zt = g_zero_one * g_one_two - g_zero_two * g_diag[1]
    cof_oo = g_diag[0] * g_diag[2] - g_zero_two * g_zero_two
    cof_ot = g_zero_one * g_zero_two - g_diag[0] * g_one_two
    cof_tt = g_diag[0] * g_diag[1] - g_zero_one * g_zero_one
    determinant = g_diag[0] * cof_zz + g_zero_one * cof_zo + g_zero_two * cof_zt
    recip = 1.0 / determinant
    omega = [
        [cof_zz * recip, cof_zo * recip, cof_zt * recip],
        [cof_zo * recip, cof_oo * recip, cof_ot * recip],
        [cof_zt * recip, cof_ot * recip, cof_tt * recip],
    ]
    traction = []
    for variant in range(3):
        traction.append(
            [
                sum((stress_b[variant, voigt[first][second]] * normal[second] for second in range(3)))
                for first in range(3)
            ]
        )
    response = []
    for variant in range(3):
        response.append(
            [
                sum((omega[first][second] * traction[variant][second] for second in range(3)))
                for first in range(3)
            ]
        )
    kernel = []
    for source in range(3):
        kernel_row = []
        for target in range(3):
            coupling = sum(
                (traction[source][first] * response[target][first] for first in range(3))
            )
            kernel_row.append(jnp.where(inside, energy[source, target] - coupling, 0.0))
        kernel.append(kernel_row)
    return kernel


def cos_sin(numer, length):
    angle = (2.0 * math.pi / length) * (numer % length).astype(jnp.float32)
    return (jnp.cos(angle), jnp.sin(angle))


def np_cos_sin(numer, length):
    angle = (2.0 * np.pi / length) * (numer % length).astype(np.float64)
    return (np.cos(angle).astype(np.float32), np.sin(angle).astype(np.float32))


def stacked_table(length):
    index = np.arange(length)
    cosine, sine = np_cos_sin(np.outer(index, index), length)
    return np.concatenate([cosine, sine], axis=0)


def block_dft8():
    size = 192
    rows_idx = lax.broadcasted_iota(jnp.int32, (size, size), 0)
    cols_idx = lax.broadcasted_iota(jnp.int32, (size, size), 1)
    same = (rows_idx // 32 == cols_idx // 32) & (rows_idx % 4 == cols_idx % 4)
    cosine, sine = cos_sin(((rows_idx // 4) % 8) * ((cols_idx // 4) % 8), 8)
    cosine = jnp.where(same, cosine, 0.0)
    sine = jnp.where(same, sine, 0.0)
    top = jnp.concatenate([cosine, -sine], axis=1)
    bottom = jnp.concatenate([sine, cosine], axis=1)
    return jnp.concatenate([top, bottom], axis=0)


def z_twiddle_table():
    rows_idx = lax.broadcasted_iota(jnp.int32, (128, 192), 0)
    cols_idx = lax.broadcasted_iota(jnp.int32, (128, 192), 1)
    return jnp.stack(cos_sin(rows_idx * ((cols_idx // 4) % 8), 1024))


def matmul(spec, left, right):
    return jnp.einsum(spec, left, right, precision=highest)


def combine_rows(product, sign):
    c_re = product[:128, :192]
    c_im = product[:128, 192:]
    s_re = product[128:, :192]
    s_im = product[128:, 192:]
    if sign < 0:
        return (c_re + s_im, c_im - s_re)
    return (c_re - s_im, c_im + s_re)


def twiddle(values, factor_cos, factor_sin):
    real_part = values[0] * factor_cos - values[1] * factor_sin
    imag_part = values[1] * factor_cos + values[0] * factor_sin
    return jnp.stack([real_part, imag_part])


def rotate_neg(values):
    return jnp.stack([values[1], -values[0]])


def rotate_pos(values):
    return jnp.stack([-values[1], values[0]])


def times_i(re, im, sign):
    return (-sign * im, sign * re)


def dft4(parts, sign):
    (r0, i0), (r1, i1), (r2, i2), (r3, i3) = parts
    ar, ai = r0 + r2, i0 + i2
    br, bi = r0 - r2, i0 - i2
    cr, ci = r1 + r3, i1 + i3
    dr, di = times_i(r1 - r3, i1 - i3, sign)
    return [(ar + cr, ai + ci), (br + dr, bi + di), (ar - cr, ai - ci), (br - dr, bi - di)]


def dft4_across(gathered, index, sign):
    (r0, i0), (r1, i1), (r2, i2), (r3, i3) = [(gathered[g, 0], gathered[g, 1]) for g in range(4)]
    ar, ai = r0 + r2, i0 + i2
    br, bi = r0 - r2, i0 - i2
    cr, ci = r1 + r3, i1 + i3
    dr, di = times_i(r1 - r3, i1 - i3, sign)
    choices = [(ar + cr, ai + ci), (br + dr, bi + di), (ar - cr, ai - ci), (br - dr, bi - di)]
    real_part = choices[3][0]
    imag_part = choices[3][1]
    for position in (2, 1, 0):
        real_part = jnp.where(index == position, choices[position][0], real_part)
        imag_part = jnp.where(index == position, choices[position][1], imag_part)
    return jnp.stack([real_part, imag_part])


def y_forward(spectral):
    parts = [(spectral[0, ..., 128 * a:128 * a + 128], spectral[1, ..., 128 * a:128 * a + 128]) for a in range(4)]
    mixed = dft4(parts, -1)
    lanes = lax.broadcasted_iota(jnp.int32, (128,), 0)
    out = []
    for k1 in range(4):
        tw_cos, tw_sin = cos_sin(lanes * k1, 512)
        re, im = mixed[k1]
        out.append(jnp.stack([re * tw_cos + im * tw_sin, im * tw_cos - re * tw_sin]))
    stacked = jnp.stack(out, axis=-2).reshape(384, 128)
    product = matmul("kb,rb->kr", stacked_table(128), stacked)
    re, im = combine_rows(product, -1)
    return jnp.concatenate([re, im], axis=1)


def y_inverse(returned):
    product = matmul("kr,bk->rb", returned, stacked_table(128))
    c_re = product[:192, :128]
    s_re = product[:192, 128:]
    c_im = product[192:, :128]
    s_im = product[192:, 128:]
    re = (c_re - s_im).reshape(3, 2, 8, 4, 128)
    im = (c_im + s_re).reshape(3, 2, 8, 4, 128)
    lanes = lax.broadcasted_iota(jnp.int32, (128,), 0)
    parts = []
    for k1 in range(4):
        tw_cos, tw_sin = cos_sin(lanes * k1, 512)
        r = re[..., k1, :]
        i = im[..., k1, :]
        parts.append((r * tw_cos - i * tw_sin, i * tw_cos + r * tw_sin))
    mixed = dft4(parts, 1)
    real_part = jnp.concatenate([m[0] for m in mixed], axis=-1)
    imag_part = jnp.concatenate([m[1] for m in mixed], axis=-1)
    return jnp.stack([real_part, imag_part])


def z_twiddle(re, im, sign):
    table = z_twiddle_table()
    tw_cos = table[0]
    tw_sin = sign * table[1]
    return jnp.concatenate([re * tw_cos - im * tw_sin, im * tw_cos + re * tw_sin], axis=1)


def shards(fields, eigenstrain, moduli):
    gy_count = lax.axis_size("gy")
    gy_index = lax.axis_index("gy")
    gz_index = lax.axis_index("gz")
    y_local = fields.shape[4]
    positions = lax.broadcasted_iota(jnp.int32, (y_local,), 0)
    spectral = dft4_across(lax.all_gather(fields, "gy", axis=0), gy_index, -1)
    residue = gy_index
    angle = 2.0 * math.pi / NY * (positions * residue % NY).astype(jnp.float32)
    phase_cos = jnp.cos(angle)
    phase_sin = jnp.sin(angle)
    spectral = twiddle(spectral, phase_cos, -phase_sin)
    slabs = y_forward(spectral)
    pencils = lax.all_to_all(slabs, "gz", split_axis=0, concat_axis=0, tiled=True)
    table = stacked_table(128)
    re, im = combine_rows(matmul("kg,gc->kc", table, pencils), -1)
    spectrum = jnp.dot(z_twiddle(re, im, -1), block_dft8(), precision=highest)
    rows_idx = lax.broadcasted_iota(jnp.int32, (128, 64), 0)
    cols_idx = lax.broadcasted_iota(jnp.int32, (128, 64), 1)
    plane = cols_idx // 32
    kz_index = rows_idx + 128 * ((cols_idx // 4) % 8)
    ky_index = residue + gy_count * (cols_idx % 4 + 4 * gz_index)
    kx_wave = plane.astype(jnp.float32) / NX
    ky_wave = signed_wave(ky_index, NY)
    kz_wave = signed_wave(kz_index, NZ)
    kernel = kernel_rows(kx_wave, ky_wave, kz_wave, eigenstrain, moduli)
    scale = 1.0 / (NY * NZ)
    spec = spectrum.reshape(128, 2, 3, 64)
    forced = jnp.stack(
        [
            jnp.stack(
                [
                    sum((kernel[source][target] * spec[:, part, target] for target in range(3))) * scale
                    for source in range(3)
                ],
                axis=1,
            )
            for part in range(2)
        ],
        axis=1,
    ).reshape(128, 384)
    back = matmul("kr,sr->ks", forced, block_dft8())
    back = z_twiddle(back[:, :192], back[:, 192:], 1)
    re, im = combine_rows(matmul("kg,gc->kc", table, back), 1)
    back = jnp.concatenate([re, im], axis=1)
    returned = lax.all_to_all(back, "gz", split_axis=0, concat_axis=0, tiled=True)
    spatial = y_inverse(returned)
    spatial = twiddle(spatial, phase_cos, phase_sin)
    result = dft4_across(lax.all_gather(spatial, "gy", axis=0), gy_index, 1)
    return result


def solution(mesh):
    in_specs = (P(None, None, None, "gz", "gy"), P(), P())
    out_specs = P(None, None, None, "gz", "gy")
    return jax.shard_map(shards, mesh=mesh, in_specs=in_specs, out_specs=out_specs, check_vma=False)
```

```python
import math

import numpy as np

import jax
import jax.numpy as jnp
from jax import lax
from jax.sharding import PartitionSpec as P

NX = 2048
NY = 2048
NZ = 1024


highest = lax.Precision.HIGHEST


def partner_2(value, axis, stride):
    mask = 2**stride
    pairs = [(source, source ^ mask) for source in range(lax.axis_size(axis))]
    return lax.ppermute(value, axis, pairs)


def signed_wave(index, length):
    return jnp.where(index < length // 2, index, index - length).astype(jnp.float32) / length


def kernel_rows(kx_wave, ky_wave, kz_wave, eigenstrain, moduli):
    constants = moduli.reshape(3, 1, 1)
    stiff_a = constants[0]
    stiff_b = constants[1]
    shear = constants[2]
    strain = eigenstrain
    trace = strain[:, 0:1] + strain[:, 1:2] + strain[:, 2:3]
    stress = jnp.concatenate(
        [
            moduli[1:2] * trace + (moduli[0:1] - moduli[1:2]) * strain[:, 0:3],
            2.0 * moduli[2:3] * strain[:, 3:6],
        ],
        axis=1,
    )
    voigt = [[0, 5, 4], [5, 1, 3], [4, 3, 2]]
    energy = sum(
        (
            stress[:, None, voigt[first][second]] * strain[None, :, voigt[first][second]]
            for first in range(3)
            for second in range(3)
        )
    )
    width = kx_wave.shape[-1]
    constants = jnp.broadcast_to(moduli[:, None], (3, width))
    stress_b = jnp.broadcast_to(stress[:, :, None], (3, 6, width))
    energy = jnp.broadcast_to(energy[:, :, None], (3, 3, width))
    constants, stress_b, energy = lax.optimization_barrier((constants, stress_b, energy))
    stiff_a = constants[0]
    stiff_b = constants[1]
    shear = constants[2]
    square = kx_wave * kx_wave + ky_wave * ky_wave + kz_wave * kz_wave
    inside = square > 0.0
    inverse = lax.rsqrt(jnp.where(inside, square, 1.0))
    normal = [kx_wave * inverse, ky_wave * inverse, kz_wave * inverse]
    g_diag = [shear + (stiff_a - shear) * normal[axis_id] * normal[axis_id] for axis_id in range(3)]
    cross_coef = stiff_b + shear
    g_zero_one = cross_coef * normal[0] * normal[1]
    g_zero_two = cross_coef * normal[0] * normal[2]
    g_one_two = cross_coef * normal[1] * normal[2]
    cof_zz = g_diag[1] * g_diag[2] - g_one_two * g_one_two
    cof_zo = g_zero_two * g_one_two - g_zero_one * g_diag[2]
    cof_zt = g_zero_one * g_one_two - g_zero_two * g_diag[1]
    cof_oo = g_diag[0] * g_diag[2] - g_zero_two * g_zero_two
    cof_ot = g_zero_one * g_zero_two - g_diag[0] * g_one_two
    cof_tt = g_diag[0] * g_diag[1] - g_zero_one * g_zero_one
    determinant = g_diag[0] * cof_zz + g_zero_one * cof_zo + g_zero_two * cof_zt
    recip = 1.0 / determinant
    omega = [
        [cof_zz * recip, cof_zo * recip, cof_zt * recip],
        [cof_zo * recip, cof_oo * recip, cof_ot * recip],
        [cof_zt * recip, cof_ot * recip, cof_tt * recip],
    ]
    traction = []
    for variant in range(3):
        traction.append(
            [
                sum((stress_b[variant, voigt[first][second]] * normal[second] for second in range(3)))
                for first in range(3)
            ]
        )
    response = []
    for variant in range(3):
        response.append(
            [
                sum((omega[first][second] * traction[variant][second] for second in range(3)))
                for first in range(3)
            ]
        )
    kernel = []
    for source in range(3):
        kernel_row = []
        for target in range(3):
            coupling = sum(
                (traction[source][first] * response[target][first] for first in range(3))
            )
            kernel_row.append(jnp.where(inside, energy[source, target] - coupling, 0.0))
        kernel.append(kernel_row)
    return kernel


def cos_sin(numer, length):
    angle = (2.0 * math.pi / length) * (numer % length).astype(jnp.float32)
    return (jnp.cos(angle), jnp.sin(angle))


def np_cos_sin(numer, length):
    angle = (2.0 * np.pi / length) * (numer % length).astype(np.float64)
    return (np.cos(angle).astype(np.float32), np.sin(angle).astype(np.float32))


def stacked_table(length):
    index = np.arange(length)
    cosine, sine = np_cos_sin(np.outer(index, index), length)
    return np.concatenate([cosine, sine], axis=0)


def block_dft8():
    size = 192
    rows_idx = lax.broadcasted_iota(jnp.int32, (size, size), 0)
    cols_idx = lax.broadcasted_iota(jnp.int32, (size, size), 1)
    same = (rows_idx // 32 == cols_idx // 32) & (rows_idx % 4 == cols_idx % 4)
    cosine, sine = cos_sin(((rows_idx // 4) % 8) * ((cols_idx // 4) % 8), 8)
    cosine = jnp.where(same, cosine, 0.0)
    sine = jnp.where(same, sine, 0.0)
    top = jnp.concatenate([cosine, -sine], axis=1)
    bottom = jnp.concatenate([sine, cosine], axis=1)
    return jnp.concatenate([top, bottom], axis=0)


def z_twiddle_table():
    rows_idx = lax.broadcasted_iota(jnp.int32, (128, 192), 0)
    cols_idx = lax.broadcasted_iota(jnp.int32, (128, 192), 1)
    return jnp.stack(cos_sin(rows_idx * ((cols_idx // 4) % 8), 1024))


def matmul(spec, left, right):
    return jnp.einsum(spec, left, right, precision=highest)


def combine_rows(product, sign):
    c_re = product[:128, :192]
    c_im = product[:128, 192:]
    s_re = product[128:, :192]
    s_im = product[128:, 192:]
    if sign < 0:
        return (c_re + s_im, c_im - s_re)
    return (c_re - s_im, c_im + s_re)


def twiddle(values, factor_cos, factor_sin):
    real_part = values[0] * factor_cos - values[1] * factor_sin
    imag_part = values[1] * factor_cos + values[0] * factor_sin
    return jnp.stack([real_part, imag_part])


def rotate_neg(values):
    return jnp.stack([values[1], -values[0]])


def rotate_pos(values):
    return jnp.stack([-values[1], values[0]])


def times_i(re, im, sign):
    return (-sign * im, sign * re)


def dft4(parts, sign):
    (r0, i0), (r1, i1), (r2, i2), (r3, i3) = parts
    ar, ai = r0 + r2, i0 + i2
    br, bi = r0 - r2, i0 - i2
    cr, ci = r1 + r3, i1 + i3
    dr, di = times_i(r1 - r3, i1 - i3, sign)
    return [(ar + cr, ai + ci), (br + dr, bi + di), (ar - cr, ai - ci), (br - dr, bi - di)]


def dft4_across(gathered, index, sign):
    (r0, i0), (r1, i1), (r2, i2), (r3, i3) = [(gathered[g, 0], gathered[g, 1]) for g in range(4)]
    ar, ai = r0 + r2, i0 + i2
    br, bi = r0 - r2, i0 - i2
    cr, ci = r1 + r3, i1 + i3
    dr, di = times_i(r1 - r3, i1 - i3, sign)
    choices = [(ar + cr, ai + ci), (br + dr, bi + di), (ar - cr, ai - ci), (br - dr, bi - di)]
    real_part = choices[3][0]
    imag_part = choices[3][1]
    for position in (2, 1, 0):
        real_part = jnp.where(index == position, choices[position][0], real_part)
        imag_part = jnp.where(index == position, choices[position][1], imag_part)
    return jnp.stack([real_part, imag_part])


def y_forward(spectral):
    parts = [(spectral[0, ..., 128 * a:128 * a + 128], spectral[1, ..., 128 * a:128 * a + 128]) for a in range(4)]
    mixed = dft4(parts, -1)
    lanes = lax.broadcasted_iota(jnp.int32, (128,), 0)
    out = []
    for k1 in range(4):
        tw_cos, tw_sin = cos_sin(lanes * k1, 512)
        re, im = mixed[k1]
        out.append(jnp.stack([re * tw_cos + im * tw_sin, im * tw_cos - re * tw_sin]))
    stacked = jnp.stack(out, axis=-2).reshape(384, 128)
    product = matmul("kb,rb->kr", stacked_table(128), stacked)
    re, im = combine_rows(product, -1)
    return jnp.concatenate([re, im], axis=1)


def y_inverse(returned):
    product = matmul("kr,bk->rb", returned, stacked_table(128))
    c_re = product[:192, :128]
    s_re = product[:192, 128:]
    c_im = product[192:, :128]
    s_im = product[192:, 128:]
    re = (c_re - s_im).reshape(3, 2, 8, 4, 128)
    im = (c_im + s_re).reshape(3, 2, 8, 4, 128)
    lanes = lax.broadcasted_iota(jnp.int32, (128,), 0)
    parts = []
    for k1 in range(4):
        tw_cos, tw_sin = cos_sin(lanes * k1, 512)
        r = re[..., k1, :]
        i = im[..., k1, :]
        parts.append((r * tw_cos - i * tw_sin, i * tw_cos + r * tw_sin))
    mixed = dft4(parts, 1)
    real_part = jnp.concatenate([m[0] for m in mixed], axis=-1)
    imag_part = jnp.concatenate([m[1] for m in mixed], axis=-1)
    return jnp.stack([real_part, imag_part])


def z_twiddle(re, im, sign):
    table = z_twiddle_table()
    tw_cos = table[0]
    tw_sin = sign * table[1]
    return jnp.concatenate([re * tw_cos - im * tw_sin, im * tw_cos + re * tw_sin], axis=1)


def shards(fields, eigenstrain, moduli):
    gy_count = lax.axis_size("gy")
    gy_index = lax.axis_index("gy")
    gz_index = lax.axis_index("gz")
    y_local = fields.shape[4]
    positions = lax.broadcasted_iota(jnp.int32, (y_local,), 0)
    spectral = dft4_across(lax.all_gather(fields, "gy", axis=0), gy_index, -1)
    residue = gy_index
    angle = 2.0 * math.pi / NY * (positions * residue % NY).astype(jnp.float32)
    phase_cos = jnp.cos(angle)
    phase_sin = jnp.sin(angle)
    spectral = twiddle(spectral, phase_cos, -phase_sin)
    slabs = y_forward(spectral)
    pencils = lax.all_to_all(slabs, "gz", split_axis=0, concat_axis=0, tiled=True)
    table = stacked_table(128)
    re, im = combine_rows(matmul("kg,gc->kc", table, pencils), -1)
    spectrum = jnp.dot(z_twiddle(re, im, -1), block_dft8(), precision=highest)
    rows_idx = lax.broadcasted_iota(jnp.int32, (128, 64), 0)
    cols_idx = lax.broadcasted_iota(jnp.int32, (128, 64), 1)
    plane = cols_idx // 32
    kz_index = rows_idx + 128 * ((cols_idx // 4) % 8)
    ky_index = residue + gy_count * (cols_idx % 4 + 4 * gz_index)
    kx_wave = plane.astype(jnp.float32) / NX
    ky_wave = signed_wave(ky_index, NY)
    kz_wave = signed_wave(kz_index, NZ)
    kernel = kernel_rows(kx_wave, ky_wave, kz_wave, eigenstrain, moduli)
    scale = 1.0 / (NY * NZ)
    spec = spectrum.reshape(128, 2, 3, 64)
    coupled = jnp.stack([jnp.stack([kernel[source][target] for target in range(3)], axis=1) for source in range(3)], axis=1)
    forced = (coupled[:, None] * spec[:, :, None]).sum(axis=3) * scale
    forced = forced.reshape(128, 384)
    back = matmul("kr,sr->ks", forced, block_dft8())
    back = z_twiddle(back[:, :192], back[:, 192:], 1)
    re, im = combine_rows(matmul("kg,gc->kc", table, back), 1)
    back = jnp.concatenate([re, im], axis=1)
    returned = lax.all_to_all(back, "gz", split_axis=0, concat_axis=0, tiled=True)
    spatial = y_inverse(returned)
    spatial = twiddle(spatial, phase_cos, phase_sin)
    result = dft4_across(lax.all_gather(spatial, "gy", axis=0), gy_index, 1)
    return result


def solution(mesh):
    in_specs = (P(None, None, None, "gz", "gy"), P(), P())
    out_specs = P(None, None, None, "gz", "gy")
    return jax.shard_map(shards, mesh=mesh, in_specs=in_specs, out_specs=out_specs, check_vma=False)
```

```python
import math

import numpy as np

import jax
import jax.numpy as jnp
from jax import lax
from jax.sharding import Mesh, PartitionSpec as P

NX = 2048
NY = 2048
NZ = 1024


highest = lax.Precision.HIGHEST


def partner_2(value, axis, stride):
    mask = 2**stride
    pairs = [(source, source ^ mask) for source in range(lax.axis_size(axis))]
    return lax.ppermute(value, axis, pairs)


def signed_wave(index, length):
    return jnp.where(index < length // 2, index, index - length).astype(jnp.float32) / length


def kernel_rows(kx_wave, ky_wave, kz_wave, eigenstrain, moduli):
    constants = moduli.reshape(3, 1, 1)
    stiff_a = constants[0]
    stiff_b = constants[1]
    shear = constants[2]
    strain = eigenstrain
    trace = strain[:, 0:1] + strain[:, 1:2] + strain[:, 2:3]
    stress = jnp.concatenate(
        [
            moduli[1:2] * trace + (moduli[0:1] - moduli[1:2]) * strain[:, 0:3],
            2.0 * moduli[2:3] * strain[:, 3:6],
        ],
        axis=1,
    )
    voigt = [[0, 5, 4], [5, 1, 3], [4, 3, 2]]
    energy = sum(
        (
            stress[:, None, voigt[first][second]] * strain[None, :, voigt[first][second]]
            for first in range(3)
            for second in range(3)
        )
    )
    width = kx_wave.shape[-1]
    constants = jnp.broadcast_to(moduli[:, None], (3, width))
    stress_b = jnp.broadcast_to(stress[:, :, None], (3, 6, width))
    energy = jnp.broadcast_to(energy[:, :, None], (3, 3, width))
    constants, stress_b, energy = lax.optimization_barrier((constants, stress_b, energy))
    stiff_a = constants[0]
    stiff_b = constants[1]
    shear = constants[2]
    square = kx_wave * kx_wave + ky_wave * ky_wave + kz_wave * kz_wave
    inside = square > 0.0
    inverse = lax.rsqrt(jnp.where(inside, square, 1.0))
    normal = [kx_wave * inverse, ky_wave * inverse, kz_wave * inverse]
    g_diag = [shear + (stiff_a - shear) * normal[axis_id] * normal[axis_id] for axis_id in range(3)]
    cross_coef = stiff_b + shear
    g_zero_one = cross_coef * normal[0] * normal[1]
    g_zero_two = cross_coef * normal[0] * normal[2]
    g_one_two = cross_coef * normal[1] * normal[2]
    cof_zz = g_diag[1] * g_diag[2] - g_one_two * g_one_two
    cof_zo = g_zero_two * g_one_two - g_zero_one * g_diag[2]
    cof_zt = g_zero_one * g_one_two - g_zero_two * g_diag[1]
    cof_oo = g_diag[0] * g_diag[2] - g_zero_two * g_zero_two
    cof_ot = g_zero_one * g_zero_two - g_diag[0] * g_one_two
    cof_tt = g_diag[0] * g_diag[1] - g_zero_one * g_zero_one
    determinant = g_diag[0] * cof_zz + g_zero_one * cof_zo + g_zero_two * cof_zt
    recip = 1.0 / determinant
    omega = [
        [cof_zz * recip, cof_zo * recip, cof_zt * recip],
        [cof_zo * recip, cof_oo * recip, cof_ot * recip],
        [cof_zt * recip, cof_ot * recip, cof_tt * recip],
    ]
    traction = []
    for variant in range(3):
        traction.append(
            [
                sum((stress_b[variant, voigt[first][second]] * normal[second] for second in range(3)))
                for first in range(3)
            ]
        )
    response = []
    for variant in range(3):
        response.append(
            [
                sum((omega[first][second] * traction[variant][second] for second in range(3)))
                for first in range(3)
            ]
        )
    kernel = []
    for source in range(3):
        kernel_row = []
        for target in range(3):
            coupling = sum(
                (traction[source][first] * response[target][first] for first in range(3))
            )
            kernel_row.append(jnp.where(inside, energy[source, target] - coupling, 0.0))
        kernel.append(kernel_row)
    return kernel


def cos_sin(numer, length):
    angle = (2.0 * math.pi / length) * (numer % length).astype(jnp.float32)
    return (jnp.cos(angle), jnp.sin(angle))


def np_cos_sin(numer, length):
    angle = (2.0 * np.pi / length) * (numer % length).astype(np.float64)
    return (np.cos(angle).astype(np.float32), np.sin(angle).astype(np.float32))


def stacked_table(length):
    index = np.arange(length)
    cosine, sine = np_cos_sin(np.outer(index, index), length)
    return np.concatenate([cosine, sine], axis=0)


def block_dft8():
    size = 192
    rows_idx = lax.broadcasted_iota(jnp.int32, (size, size), 0)
    cols_idx = lax.broadcasted_iota(jnp.int32, (size, size), 1)
    same = (rows_idx // 32 == cols_idx // 32) & (rows_idx % 4 == cols_idx % 4)
    cosine, sine = cos_sin(((rows_idx // 4) % 8) * ((cols_idx // 4) % 8), 8)
    cosine = jnp.where(same, cosine, 0.0)
    sine = jnp.where(same, sine, 0.0)
    top = jnp.concatenate([cosine, -sine], axis=1)
    bottom = jnp.concatenate([sine, cosine], axis=1)
    return jnp.concatenate([top, bottom], axis=0)


def z_twiddle_table():
    rows_idx = lax.broadcasted_iota(jnp.int32, (128, 192), 0)
    cols_idx = lax.broadcasted_iota(jnp.int32, (128, 192), 1)
    return jnp.stack(cos_sin(rows_idx * ((cols_idx // 4) % 8), 1024))


def matmul(spec, left, right):
    return jnp.einsum(spec, left, right, precision=highest)


def combine_rows(product, sign):
    c_re = product[:128, :192]
    c_im = product[:128, 192:]
    s_re = product[128:, :192]
    s_im = product[128:, 192:]
    if sign < 0:
        return (c_re + s_im, c_im - s_re)
    return (c_re - s_im, c_im + s_re)


def twiddle(values, factor_cos, factor_sin):
    real_part = values[0] * factor_cos - values[1] * factor_sin
    imag_part = values[1] * factor_cos + values[0] * factor_sin
    return jnp.stack([real_part, imag_part])


def rotate_neg(values):
    return jnp.stack([values[1], -values[0]])


def rotate_pos(values):
    return jnp.stack([-values[1], values[0]])


def times_i(re, im, sign):
    return (-sign * im, sign * re)


def dft4(parts, sign):
    (r0, i0), (r1, i1), (r2, i2), (r3, i3) = parts
    ar, ai = r0 + r2, i0 + i2
    br, bi = r0 - r2, i0 - i2
    cr, ci = r1 + r3, i1 + i3
    dr, di = times_i(r1 - r3, i1 - i3, sign)
    return [(ar + cr, ai + ci), (br + dr, bi + di), (ar - cr, ai - ci), (br - dr, bi - di)]


def dft4_across(gathered, index, sign):
    (r0, i0), (r1, i1), (r2, i2), (r3, i3) = [(gathered[g, 0], gathered[g, 1]) for g in range(4)]
    ar, ai = r0 + r2, i0 + i2
    br, bi = r0 - r2, i0 - i2
    cr, ci = r1 + r3, i1 + i3
    dr, di = times_i(r1 - r3, i1 - i3, sign)
    choices = [(ar + cr, ai + ci), (br + dr, bi + di), (ar - cr, ai - ci), (br - dr, bi - di)]
    real_part = choices[3][0]
    imag_part = choices[3][1]
    for position in (2, 1, 0):
        real_part = jnp.where(index == position, choices[position][0], real_part)
        imag_part = jnp.where(index == position, choices[position][1], imag_part)
    return jnp.stack([real_part, imag_part])


def y_forward(spectral):
    parts = [(spectral[0, ..., 128 * a:128 * a + 128], spectral[1, ..., 128 * a:128 * a + 128]) for a in range(4)]
    mixed = dft4(parts, -1)
    lanes = lax.broadcasted_iota(jnp.int32, (128,), 0)
    out = []
    for k1 in range(4):
        tw_cos, tw_sin = cos_sin(lanes * k1, 512)
        re, im = mixed[k1]
        out.append(jnp.stack([re * tw_cos + im * tw_sin, im * tw_cos - re * tw_sin]))
    stacked = jnp.stack(out, axis=-2).reshape(384, 128)
    product = matmul("kb,rb->kr", stacked_table(128), stacked)
    re, im = combine_rows(product, -1)
    return jnp.concatenate([re, im], axis=1)


def y_inverse(returned):
    product = matmul("kr,bk->rb", returned, stacked_table(128))
    c_re = product[:192, :128]
    s_re = product[:192, 128:]
    c_im = product[192:, :128]
    s_im = product[192:, 128:]
    re = (c_re - s_im).reshape(3, 2, 8, 4, 128)
    im = (c_im + s_re).reshape(3, 2, 8, 4, 128)
    lanes = lax.broadcasted_iota(jnp.int32, (128,), 0)
    parts = []
    for k1 in range(4):
        tw_cos, tw_sin = cos_sin(lanes * k1, 512)
        r = re[..., k1, :]
        i = im[..., k1, :]
        parts.append((r * tw_cos - i * tw_sin, i * tw_cos + r * tw_sin))
    mixed = dft4(parts, 1)
    real_part = jnp.concatenate([m[0] for m in mixed], axis=-1)
    imag_part = jnp.concatenate([m[1] for m in mixed], axis=-1)
    return jnp.stack([real_part, imag_part])


def z_twiddle(re, im, sign):
    table = z_twiddle_table()
    tw_cos = table[0]
    tw_sin = sign * table[1]
    return jnp.concatenate([re * tw_cos - im * tw_sin, im * tw_cos + re * tw_sin], axis=1)


def shards(fields, eigenstrain, moduli):
    gy_count = lax.axis_size("gy_chip") * lax.axis_size("gy_core")
    gy_index = lax.axis_index("gy_chip") * lax.axis_size("gy_core") + lax.axis_index("gy_core")
    gz_index = lax.axis_index("gz")
    y_local = fields.shape[4]
    positions = lax.broadcasted_iota(jnp.int32, (y_local,), 0)
    spectral = dft4_across(lax.all_gather(fields, ("gy_chip", "gy_core"), axis=0), gy_index, -1)
    residue = gy_index
    angle = 2.0 * math.pi / NY * (positions * residue % NY).astype(jnp.float32)
    phase_cos = jnp.cos(angle)
    phase_sin = jnp.sin(angle)
    spectral = twiddle(spectral, phase_cos, -phase_sin)
    slabs = y_forward(spectral)
    pencils = lax.all_to_all(slabs, "gz", split_axis=0, concat_axis=0, tiled=True)
    table = stacked_table(128)
    re, im = combine_rows(matmul("kg,gc->kc", table, pencils), -1)
    spectrum = jnp.dot(z_twiddle(re, im, -1), block_dft8(), precision=highest)
    rows_idx = lax.broadcasted_iota(jnp.int32, (128, 64), 0)
    cols_idx = lax.broadcasted_iota(jnp.int32, (128, 64), 1)
    plane = cols_idx // 32
    kz_index = rows_idx + 128 * ((cols_idx // 4) % 8)
    ky_index = residue + gy_count * (cols_idx % 4 + 4 * gz_index)
    kx_wave = plane.astype(jnp.float32) / NX
    ky_wave = signed_wave(ky_index, NY)
    kz_wave = signed_wave(kz_index, NZ)
    kernel = kernel_rows(kx_wave, ky_wave, kz_wave, eigenstrain, moduli)
    scale = 1.0 / (NY * NZ)
    spec = spectrum.reshape(128, 2, 3, 64)
    coupled = jnp.stack([jnp.stack([kernel[source][target] for target in range(3)], axis=1) for source in range(3)], axis=1)
    forced = (coupled[:, None] * spec[:, :, None]).sum(axis=3) * scale
    forced = forced.reshape(128, 384)
    back = matmul("kr,sr->ks", forced, block_dft8())
    back = z_twiddle(back[:, :192], back[:, 192:], 1)
    re, im = combine_rows(matmul("kg,gc->kc", table, back), 1)
    back = jnp.concatenate([re, im], axis=1)
    returned = lax.all_to_all(back, "gz", split_axis=0, concat_axis=0, tiled=True)
    spatial = y_inverse(returned)
    spatial = twiddle(spatial, phase_cos, phase_sin)
    gathered = lax.all_gather(spatial, ("gy_core", "gy_chip"), axis=0)
    result = dft4_across(gathered[jnp.array([0, 2, 1, 3])], gy_index, 1)
    return result


def solution(mesh):
    chips = mesh.shape["gy"] // 2
    split = Mesh(mesh.devices.reshape(chips, 2, mesh.shape["gz"]), ("gy_chip", "gy_core", "gz"))
    block = P(None, None, None, "gz", ("gy_chip", "gy_core"))
    in_specs = (block, P(), P())
    return jax.shard_map(shards, mesh=split, in_specs=in_specs, out_specs=block, check_vma=False)
```

```python
import math

import numpy as np

import jax
import jax.numpy as jnp
from jax import lax
from jax.sharding import PartitionSpec as P

NX = 2048
NY = 2048
NZ = 1024


highest = lax.Precision.HIGHEST


def partner_2(value, axis, stride):
    mask = 2**stride
    pairs = [(source, source ^ mask) for source in range(lax.axis_size(axis))]
    return lax.ppermute(value, axis, pairs)


def signed_wave(index, length):
    return jnp.where(index < length // 2, index, index - length).astype(jnp.float32) / length


def kernel_rows(kx_wave, ky_wave, kz_wave, eigenstrain, moduli):
    constants = moduli.reshape(3, 1, 1)
    stiff_a = constants[0]
    stiff_b = constants[1]
    shear = constants[2]
    strain = eigenstrain
    trace = strain[:, 0:1] + strain[:, 1:2] + strain[:, 2:3]
    stress = jnp.concatenate(
        [
            moduli[1:2] * trace + (moduli[0:1] - moduli[1:2]) * strain[:, 0:3],
            2.0 * moduli[2:3] * strain[:, 3:6],
        ],
        axis=1,
    )
    voigt = [[0, 5, 4], [5, 1, 3], [4, 3, 2]]
    energy = sum(
        (
            stress[:, None, voigt[first][second]] * strain[None, :, voigt[first][second]]
            for first in range(3)
            for second in range(3)
        )
    )
    width = kx_wave.shape[-1]
    constants = jnp.broadcast_to(moduli[:, None], (3, width))
    stress_b = jnp.broadcast_to(stress[:, :, None], (3, 6, width))
    energy = jnp.broadcast_to(energy[:, :, None], (3, 3, width))
    constants, stress_b, energy = lax.optimization_barrier((constants, stress_b, energy))
    stiff_a = constants[0]
    stiff_b = constants[1]
    shear = constants[2]
    square = kx_wave * kx_wave + ky_wave * ky_wave + kz_wave * kz_wave
    inside = square > 0.0
    inverse = lax.rsqrt(jnp.where(inside, square, 1.0))
    normal = [kx_wave * inverse, ky_wave * inverse, kz_wave * inverse]
    g_diag = [shear + (stiff_a - shear) * normal[axis_id] * normal[axis_id] for axis_id in range(3)]
    cross_coef = stiff_b + shear
    g_zero_one = cross_coef * normal[0] * normal[1]
    g_zero_two = cross_coef * normal[0] * normal[2]
    g_one_two = cross_coef * normal[1] * normal[2]
    cof_zz = g_diag[1] * g_diag[2] - g_one_two * g_one_two
    cof_zo = g_zero_two * g_one_two - g_zero_one * g_diag[2]
    cof_zt = g_zero_one * g_one_two - g_zero_two * g_diag[1]
    cof_oo = g_diag[0] * g_diag[2] - g_zero_two * g_zero_two
    cof_ot = g_zero_one * g_zero_two - g_diag[0] * g_one_two
    cof_tt = g_diag[0] * g_diag[1] - g_zero_one * g_zero_one
    determinant = g_diag[0] * cof_zz + g_zero_one * cof_zo + g_zero_two * cof_zt
    recip = 1.0 / determinant
    omega = [
        [cof_zz * recip, cof_zo * recip, cof_zt * recip],
        [cof_zo * recip, cof_oo * recip, cof_ot * recip],
        [cof_zt * recip, cof_ot * recip, cof_tt * recip],
    ]
    traction = []
    for variant in range(3):
        traction.append(
            [
                sum((stress_b[variant, voigt[first][second]] * normal[second] for second in range(3)))
                for first in range(3)
            ]
        )
    response = []
    for variant in range(3):
        response.append(
            [
                sum((omega[first][second] * traction[variant][second] for second in range(3)))
                for first in range(3)
            ]
        )
    kernel = []
    for source in range(3):
        kernel_row = []
        for target in range(3):
            coupling = sum(
                (traction[source][first] * response[target][first] for first in range(3))
            )
            kernel_row.append(jnp.where(inside, energy[source, target] - coupling, 0.0))
        kernel.append(kernel_row)
    return kernel


def cos_sin(numer, length):
    angle = (2.0 * math.pi / length) * (numer % length).astype(jnp.float32)
    return (jnp.cos(angle), jnp.sin(angle))


def np_cos_sin(numer, length):
    angle = (2.0 * np.pi / length) * (numer % length).astype(np.float64)
    return (np.cos(angle).astype(np.float32), np.sin(angle).astype(np.float32))


def stacked_table(length):
    index = np.arange(length)
    cosine, sine = np_cos_sin(np.outer(index, index), length)
    return np.concatenate([cosine, sine], axis=0)


def block_dft8():
    size = 192
    rows_idx = lax.broadcasted_iota(jnp.int32, (size, size), 0)
    cols_idx = lax.broadcasted_iota(jnp.int32, (size, size), 1)
    same = (rows_idx // 32 == cols_idx // 32) & (rows_idx % 4 == cols_idx % 4)
    cosine, sine = cos_sin(((rows_idx // 4) % 8) * ((cols_idx // 4) % 8), 8)
    cosine = jnp.where(same, cosine, 0.0)
    sine = jnp.where(same, sine, 0.0)
    top = jnp.concatenate([cosine, -sine], axis=1)
    bottom = jnp.concatenate([sine, cosine], axis=1)
    return jnp.concatenate([top, bottom], axis=0)


def dft8_apply(values, inverse):
    matrix = block_dft8_np()
    if inverse:
        matrix = matrix.T
    unit = np.where(np.abs(matrix) > 0.9, np.sign(matrix), 0.0)
    half = np.where((np.abs(matrix) > 0.5) & (np.abs(matrix) < 0.9), np.sign(matrix), 0.0)
    table = jnp.asarray(np.concatenate([unit, half], axis=1), jnp.bfloat16)
    first = lax.reduce_precision(values, exponent_bits=8, mantissa_bits=7)
    rest = values - first
    second = lax.reduce_precision(rest, exponent_bits=8, mantissa_bits=7)
    third = rest - second
    parts = jnp.concatenate([first, second, third], axis=0).astype(jnp.bfloat16)
    product = jnp.dot(parts, table, preferred_element_type=jnp.float32)
    summed = product[:128] + product[128:256] + product[256:]
    return summed[:, :384] + np.float32(math.sqrt(0.5)) * summed[:, 384:]


def block_dft8_np():
    size = 192
    rows_idx = np.arange(size)[:, None]
    cols_idx = np.arange(size)[None, :]
    same = (rows_idx // 32 == cols_idx // 32) & (rows_idx % 4 == cols_idx % 4)
    cosine, sine = np_cos_sin(((rows_idx // 4) % 8) * ((cols_idx // 4) % 8), 8)
    cosine = np.where(same, cosine, 0.0).astype(np.float32)
    sine = np.where(same, sine, 0.0).astype(np.float32)
    top = np.concatenate([cosine, -sine], axis=1)
    bottom = np.concatenate([sine, cosine], axis=1)
    return np.concatenate([top, bottom], axis=0)


def z_twiddle_table():
    rows_idx = lax.broadcasted_iota(jnp.int32, (128, 192), 0)
    cols_idx = lax.broadcasted_iota(jnp.int32, (128, 192), 1)
    return jnp.stack(cos_sin(rows_idx * ((cols_idx // 4) % 8), 1024))


def matmul(spec, left, right):
    return jnp.einsum(spec, left, right, precision=highest)


def combine_rows(product, sign):
    c_re = product[:128, :192]
    c_im = product[:128, 192:]
    s_re = product[128:, :192]
    s_im = product[128:, 192:]
    if sign < 0:
        return (c_re + s_im, c_im - s_re)
    return (c_re - s_im, c_im + s_re)


def twiddle(values, factor_cos, factor_sin):
    real_part = values[0] * factor_cos - values[1] * factor_sin
    imag_part = values[1] * factor_cos + values[0] * factor_sin
    return jnp.stack([real_part, imag_part])


def rotate_neg(values):
    return jnp.stack([values[1], -values[0]])


def rotate_pos(values):
    return jnp.stack([-values[1], values[0]])


def times_i(re, im, sign):
    return (-sign * im, sign * re)


def dft4(parts, sign):
    (r0, i0), (r1, i1), (r2, i2), (r3, i3) = parts
    ar, ai = r0 + r2, i0 + i2
    br, bi = r0 - r2, i0 - i2
    cr, ci = r1 + r3, i1 + i3
    dr, di = times_i(r1 - r3, i1 - i3, sign)
    return [(ar + cr, ai + ci), (br + dr, bi + di), (ar - cr, ai - ci), (br - dr, bi - di)]


def dft4_across(gathered, index, sign):
    (r0, i0), (r1, i1), (r2, i2), (r3, i3) = [(gathered[g, 0], gathered[g, 1]) for g in range(4)]
    ar, ai = r0 + r2, i0 + i2
    br, bi = r0 - r2, i0 - i2
    cr, ci = r1 + r3, i1 + i3
    dr, di = times_i(r1 - r3, i1 - i3, sign)
    choices = [(ar + cr, ai + ci), (br + dr, bi + di), (ar - cr, ai - ci), (br - dr, bi - di)]
    real_part = choices[3][0]
    imag_part = choices[3][1]
    for position in (2, 1, 0):
        real_part = jnp.where(index == position, choices[position][0], real_part)
        imag_part = jnp.where(index == position, choices[position][1], imag_part)
    return jnp.stack([real_part, imag_part])


def y_forward(spectral):
    parts = [(spectral[0, ..., 128 * a:128 * a + 128], spectral[1, ..., 128 * a:128 * a + 128]) for a in range(4)]
    mixed = dft4(parts, -1)
    lanes = lax.broadcasted_iota(jnp.int32, (128,), 0)
    out = []
    for k1 in range(4):
        tw_cos, tw_sin = cos_sin(lanes * k1, 512)
        re, im = mixed[k1]
        out.append(jnp.stack([re * tw_cos + im * tw_sin, im * tw_cos - re * tw_sin]))
    stacked = jnp.stack(out, axis=-2).reshape(384, 128)
    product = matmul("kb,rb->kr", stacked_table(128), stacked)
    re, im = combine_rows(product, -1)
    return jnp.concatenate([re, im], axis=1)


def y_inverse(returned):
    product = matmul("kr,bk->rb", returned, stacked_table(128))
    c_re = product[:192, :128]
    s_re = product[:192, 128:]
    c_im = product[192:, :128]
    s_im = product[192:, 128:]
    re = (c_re - s_im).reshape(3, 2, 8, 4, 128)
    im = (c_im + s_re).reshape(3, 2, 8, 4, 128)
    lanes = lax.broadcasted_iota(jnp.int32, (128,), 0)
    parts = []
    for k1 in range(4):
        tw_cos, tw_sin = cos_sin(lanes * k1, 512)
        r = re[..., k1, :]
        i = im[..., k1, :]
        parts.append((r * tw_cos - i * tw_sin, i * tw_cos + r * tw_sin))
    mixed = dft4(parts, 1)
    real_part = jnp.concatenate([m[0] for m in mixed], axis=-1)
    imag_part = jnp.concatenate([m[1] for m in mixed], axis=-1)
    return jnp.stack([real_part, imag_part])


def z_twiddle(re, im, sign):
    table = z_twiddle_table()
    tw_cos = table[0]
    tw_sin = sign * table[1]
    return jnp.concatenate([re * tw_cos - im * tw_sin, im * tw_cos + re * tw_sin], axis=1)


def shards(fields, eigenstrain, moduli):
    gy_count = lax.axis_size("gy")
    gy_index = lax.axis_index("gy")
    gz_index = lax.axis_index("gz")
    y_local = fields.shape[4]
    positions = lax.broadcasted_iota(jnp.int32, (y_local,), 0)
    spectral = dft4_across(lax.all_gather(fields, "gy", axis=0), gy_index, -1)
    residue = gy_index
    angle = 2.0 * math.pi / NY * (positions * residue % NY).astype(jnp.float32)
    phase_cos = jnp.cos(angle)
    phase_sin = jnp.sin(angle)
    spectral = twiddle(spectral, phase_cos, -phase_sin)
    slabs = y_forward(spectral)
    pencils = lax.all_to_all(slabs, "gz", split_axis=0, concat_axis=0, tiled=True)
    table = stacked_table(128)
    re, im = combine_rows(matmul("kg,gc->kc", table, pencils), -1)
    spectrum = dft8_apply(z_twiddle(re, im, -1), False)
    rows_idx = lax.broadcasted_iota(jnp.int32, (128, 64), 0)
    cols_idx = lax.broadcasted_iota(jnp.int32, (128, 64), 1)
    plane = cols_idx // 32
    kz_index = rows_idx + 128 * ((cols_idx // 4) % 8)
    ky_index = residue + gy_count * (cols_idx % 4 + 4 * gz_index)
    kx_wave = plane.astype(jnp.float32) / NX
    ky_wave = signed_wave(ky_index, NY)
    kz_wave = signed_wave(kz_index, NZ)
    kernel = kernel_rows(kx_wave, ky_wave, kz_wave, eigenstrain, moduli)
    scale = 1.0 / (NY * NZ)
    spec = spectrum.reshape(128, 2, 3, 64)
    coupled = jnp.stack([jnp.stack([kernel[source][target] for target in range(3)], axis=1) for source in range(3)], axis=1)
    forced = (coupled[:, None] * spec[:, :, None]).sum(axis=3) * scale
    forced = forced.reshape(128, 384)
    back = dft8_apply(forced, True)
    back = z_twiddle(back[:, :192], back[:, 192:], 1)
    re, im = combine_rows(matmul("kg,gc->kc", table, back), 1)
    back = jnp.concatenate([re, im], axis=1)
    returned = lax.all_to_all(back, "gz", split_axis=0, concat_axis=0, tiled=True)
    spatial = y_inverse(returned)
    spatial = twiddle(spatial, phase_cos, phase_sin)
    result = dft4_across(lax.all_gather(spatial, "gy", axis=0), gy_index, 1)
    return result


def solution(mesh):
    in_specs = (P(None, None, None, "gz", "gy"), P(), P())
    out_specs = P(None, None, None, "gz", "gy")
    return jax.shard_map(shards, mesh=mesh, in_specs=in_specs, out_specs=out_specs, check_vma=False)
```

```python
import math

import numpy as np

import jax
import jax.numpy as jnp
from jax import lax
from jax.sharding import PartitionSpec as P

NX = 2048
NY = 2048
NZ = 1024


highest = lax.Precision.HIGHEST


def partner_2(value, axis, stride):
    mask = 2**stride
    pairs = [(source, source ^ mask) for source in range(lax.axis_size(axis))]
    return lax.ppermute(value, axis, pairs)


def signed_wave(index, length):
    return jnp.where(index < length // 2, index, index - length).astype(jnp.float32) / length


def kernel_rows(kx_wave, ky_wave, kz_wave, eigenstrain, moduli):
    constants = moduli.reshape(3, 1, 1)
    stiff_a = constants[0]
    stiff_b = constants[1]
    shear = constants[2]
    strain = eigenstrain
    trace = strain[:, 0:1] + strain[:, 1:2] + strain[:, 2:3]
    stress = jnp.concatenate(
        [
            moduli[1:2] * trace + (moduli[0:1] - moduli[1:2]) * strain[:, 0:3],
            2.0 * moduli[2:3] * strain[:, 3:6],
        ],
        axis=1,
    )
    voigt = [[0, 5, 4], [5, 1, 3], [4, 3, 2]]
    energy = sum(
        (
            stress[:, None, voigt[first][second]] * strain[None, :, voigt[first][second]]
            for first in range(3)
            for second in range(3)
        )
    )
    width = kx_wave.shape[-1]
    constants = jnp.broadcast_to(moduli[:, None], (3, width))
    stress_b = jnp.broadcast_to(stress[:, :, None], (3, 6, width))
    energy = jnp.broadcast_to(energy[:, :, None], (3, 3, width))
    constants, stress_b, energy = lax.optimization_barrier((constants, stress_b, energy))
    stiff_a = constants[0]
    stiff_b = constants[1]
    shear = constants[2]
    square = kx_wave * kx_wave + ky_wave * ky_wave + kz_wave * kz_wave
    inside = square > 0.0
    inverse = lax.rsqrt(jnp.where(inside, square, 1.0))
    normal = [kx_wave * inverse, ky_wave * inverse, kz_wave * inverse]
    g_diag = [shear + (stiff_a - shear) * normal[axis_id] * normal[axis_id] for axis_id in range(3)]
    cross_coef = stiff_b + shear
    g_zero_one = cross_coef * normal[0] * normal[1]
    g_zero_two = cross_coef * normal[0] * normal[2]
    g_one_two = cross_coef * normal[1] * normal[2]
    cof_zz = g_diag[1] * g_diag[2] - g_one_two * g_one_two
    cof_zo = g_zero_two * g_one_two - g_zero_one * g_diag[2]
    cof_zt = g_zero_one * g_one_two - g_zero_two * g_diag[1]
    cof_oo = g_diag[0] * g_diag[2] - g_zero_two * g_zero_two
    cof_ot = g_zero_one * g_zero_two - g_diag[0] * g_one_two
    cof_tt = g_diag[0] * g_diag[1] - g_zero_one * g_zero_one
    determinant = g_diag[0] * cof_zz + g_zero_one * cof_zo + g_zero_two * cof_zt
    recip = 1.0 / determinant
    omega = [
        [cof_zz * recip, cof_zo * recip, cof_zt * recip],
        [cof_zo * recip, cof_oo * recip, cof_ot * recip],
        [cof_zt * recip, cof_ot * recip, cof_tt * recip],
    ]
    traction = []
    for variant in range(3):
        traction.append(
            [
                sum((stress_b[variant, voigt[first][second]] * normal[second] for second in range(3)))
                for first in range(3)
            ]
        )
    response = []
    for variant in range(3):
        response.append(
            [
                sum((omega[first][second] * traction[variant][second] for second in range(3)))
                for first in range(3)
            ]
        )
    kernel = []
    for source in range(3):
        kernel_row = []
        for target in range(3):
            coupling = sum(
                (traction[source][first] * response[target][first] for first in range(3))
            )
            kernel_row.append(jnp.where(inside, energy[source, target] - coupling, 0.0))
        kernel.append(kernel_row)
    return kernel


def cos_sin(numer, length):
    angle = (2.0 * math.pi / length) * (numer % length).astype(jnp.float32)
    return (jnp.cos(angle), jnp.sin(angle))


def np_cos_sin(numer, length):
    angle = (2.0 * np.pi / length) * (numer % length).astype(np.float64)
    return (np.cos(angle).astype(np.float32), np.sin(angle).astype(np.float32))


def stacked_table(length):
    index = np.arange(length)
    cosine, sine = np_cos_sin(np.outer(index, index), length)
    return np.concatenate([cosine, sine], axis=0)


def block_dft8():
    size = 192
    rows_idx = lax.broadcasted_iota(jnp.int32, (size, size), 0)
    cols_idx = lax.broadcasted_iota(jnp.int32, (size, size), 1)
    same = (rows_idx // 32 == cols_idx // 32) & (rows_idx % 4 == cols_idx % 4)
    cosine, sine = cos_sin(((rows_idx // 4) % 8) * ((cols_idx // 4) % 8), 8)
    cosine = jnp.where(same, cosine, 0.0)
    sine = jnp.where(same, sine, 0.0)
    top = jnp.concatenate([cosine, -sine], axis=1)
    bottom = jnp.concatenate([sine, cosine], axis=1)
    return jnp.concatenate([top, bottom], axis=0)


def dft8_parts(inverse):
    rows = lax.broadcasted_iota(jnp.int32, (384, 384), 0)
    cols = lax.broadcasted_iota(jnp.int32, (384, 384), 1)
    if inverse:
        rows, cols = cols, rows
    inner_r = rows % 192
    inner_c = cols % 192
    same = (inner_r // 32 == inner_c // 32) & (inner_r % 4 == inner_c % 4)
    m = (((inner_r // 4) % 8) * ((inner_c // 4) % 8)) % 8

    def pick(plus, minus):
        hit_plus = (m == plus[0]) | (m == plus[-1])
        hit_minus = (m == minus[0]) | (m == minus[-1])
        return jnp.where(hit_plus, 1.0, jnp.where(hit_minus, -1.0, 0.0))

    diag = rows // 192 == cols // 192
    sign = jnp.where(rows // 192 == 0, -1.0, 1.0)
    unit = jnp.where(same, jnp.where(diag, pick((0,), (4,)), sign * pick((2,), (6,))), 0.0)
    half = jnp.where(same, jnp.where(diag, pick((1, 7), (3, 5)), sign * pick((1, 3), (5, 7))), 0.0)
    return jnp.concatenate([unit, half], axis=1).astype(jnp.bfloat16)


def dft8_apply(values, inverse):
    table = dft8_parts(inverse)
    first = lax.reduce_precision(values, exponent_bits=8, mantissa_bits=7)
    rest = values - first
    second = lax.reduce_precision(rest, exponent_bits=8, mantissa_bits=7)
    third = rest - second
    parts = jnp.concatenate([first, second, third], axis=0).astype(jnp.bfloat16)
    product = jnp.dot(parts, table, preferred_element_type=jnp.float32)
    summed = product[:128] + product[128:256] + product[256:]
    return summed[:, :384] + np.float32(math.sqrt(0.5)) * summed[:, 384:]


def block_dft8_np():
    size = 192
    rows_idx = np.arange(size)[:, None]
    cols_idx = np.arange(size)[None, :]
    same = (rows_idx // 32 == cols_idx // 32) & (rows_idx % 4 == cols_idx % 4)
    cosine, sine = np_cos_sin(((rows_idx // 4) % 8) * ((cols_idx // 4) % 8), 8)
    cosine = np.where(same, cosine, 0.0).astype(np.float32)
    sine = np.where(same, sine, 0.0).astype(np.float32)
    top = np.concatenate([cosine, -sine], axis=1)
    bottom = np.concatenate([sine, cosine], axis=1)
    return np.concatenate([top, bottom], axis=0)


def z_twiddle_table():
    rows_idx = lax.broadcasted_iota(jnp.int32, (128, 192), 0)
    cols_idx = lax.broadcasted_iota(jnp.int32, (128, 192), 1)
    return jnp.stack(cos_sin(rows_idx * ((cols_idx // 4) % 8), 1024))


def matmul(spec, left, right):
    return jnp.einsum(spec, left, right, precision=highest)


def combine_rows(product, sign):
    c_re = product[:128, :192]
    c_im = product[:128, 192:]
    s_re = product[128:, :192]
    s_im = product[128:, 192:]
    if sign < 0:
        return (c_re + s_im, c_im - s_re)
    return (c_re - s_im, c_im + s_re)


def twiddle(values, factor_cos, factor_sin):
    real_part = values[0] * factor_cos - values[1] * factor_sin
    imag_part = values[1] * factor_cos + values[0] * factor_sin
    return jnp.stack([real_part, imag_part])


def rotate_neg(values):
    return jnp.stack([values[1], -values[0]])


def rotate_pos(values):
    return jnp.stack([-values[1], values[0]])


def times_i(re, im, sign):
    return (-sign * im, sign * re)


def dft4(parts, sign):
    (r0, i0), (r1, i1), (r2, i2), (r3, i3) = parts
    ar, ai = r0 + r2, i0 + i2
    br, bi = r0 - r2, i0 - i2
    cr, ci = r1 + r3, i1 + i3
    dr, di = times_i(r1 - r3, i1 - i3, sign)
    return [(ar + cr, ai + ci), (br + dr, bi + di), (ar - cr, ai - ci), (br - dr, bi - di)]


def dft4_across(gathered, index, sign):
    (r0, i0), (r1, i1), (r2, i2), (r3, i3) = [(gathered[g, 0], gathered[g, 1]) for g in range(4)]
    ar, ai = r0 + r2, i0 + i2
    br, bi = r0 - r2, i0 - i2
    cr, ci = r1 + r3, i1 + i3
    dr, di = times_i(r1 - r3, i1 - i3, sign)
    choices = [(ar + cr, ai + ci), (br + dr, bi + di), (ar - cr, ai - ci), (br - dr, bi - di)]
    real_part = choices[3][0]
    imag_part = choices[3][1]
    for position in (2, 1, 0):
        real_part = jnp.where(index == position, choices[position][0], real_part)
        imag_part = jnp.where(index == position, choices[position][1], imag_part)
    return jnp.stack([real_part, imag_part])


def y_forward(spectral):
    parts = [(spectral[0, ..., 128 * a:128 * a + 128], spectral[1, ..., 128 * a:128 * a + 128]) for a in range(4)]
    mixed = dft4(parts, -1)
    lanes = lax.broadcasted_iota(jnp.int32, (128,), 0)
    out = []
    for k1 in range(4):
        tw_cos, tw_sin = cos_sin(lanes * k1, 512)
        re, im = mixed[k1]
        out.append(jnp.stack([re * tw_cos + im * tw_sin, im * tw_cos - re * tw_sin]))
    stacked = jnp.stack(out, axis=-2).reshape(384, 128)
    product = matmul("kb,rb->kr", stacked_table(128), stacked)
    re, im = combine_rows(product, -1)
    return jnp.concatenate([re, im], axis=1)


def y_inverse(returned):
    product = matmul("kr,bk->rb", returned, stacked_table(128))
    c_re = product[:192, :128]
    s_re = product[:192, 128:]
    c_im = product[192:, :128]
    s_im = product[192:, 128:]
    re = (c_re - s_im).reshape(3, 2, 8, 4, 128)
    im = (c_im + s_re).reshape(3, 2, 8, 4, 128)
    lanes = lax.broadcasted_iota(jnp.int32, (128,), 0)
    parts = []
    for k1 in range(4):
        tw_cos, tw_sin = cos_sin(lanes * k1, 512)
        r = re[..., k1, :]
        i = im[..., k1, :]
        parts.append((r * tw_cos - i * tw_sin, i * tw_cos + r * tw_sin))
    mixed = dft4(parts, 1)
    real_part = jnp.concatenate([m[0] for m in mixed], axis=-1)
    imag_part = jnp.concatenate([m[1] for m in mixed], axis=-1)
    return jnp.stack([real_part, imag_part])


def z_twiddle(re, im, sign):
    table = z_twiddle_table()
    tw_cos = table[0]
    tw_sin = sign * table[1]
    return jnp.concatenate([re * tw_cos - im * tw_sin, im * tw_cos + re * tw_sin], axis=1)


def shards(fields, eigenstrain, moduli):
    gy_count = lax.axis_size("gy")
    gy_index = lax.axis_index("gy")
    gz_index = lax.axis_index("gz")
    y_local = fields.shape[4]
    positions = lax.broadcasted_iota(jnp.int32, (y_local,), 0)
    spectral = dft4_across(lax.all_gather(fields, "gy", axis=0), gy_index, -1)
    residue = gy_index
    angle = 2.0 * math.pi / NY * (positions * residue % NY).astype(jnp.float32)
    phase_cos = jnp.cos(angle)
    phase_sin = jnp.sin(angle)
    spectral = twiddle(spectral, phase_cos, -phase_sin)
    slabs = y_forward(spectral)
    pencils = lax.all_to_all(slabs, "gz", split_axis=0, concat_axis=0, tiled=True)
    table = stacked_table(128)
    re, im = combine_rows(matmul("kg,gc->kc", table, pencils), -1)
    spectrum = dft8_apply(z_twiddle(re, im, -1), False)
    rows_idx = lax.broadcasted_iota(jnp.int32, (128, 64), 0)
    cols_idx = lax.broadcasted_iota(jnp.int32, (128, 64), 1)
    plane = cols_idx // 32
    kz_index = rows_idx + 128 * ((cols_idx // 4) % 8)
    ky_index = residue + gy_count * (cols_idx % 4 + 4 * gz_index)
    kx_wave = plane.astype(jnp.float32) / NX
    ky_wave = signed_wave(ky_index, NY)
    kz_wave = signed_wave(kz_index, NZ)
    kernel = kernel_rows(kx_wave, ky_wave, kz_wave, eigenstrain, moduli)
    scale = 1.0 / (NY * NZ)
    spec = spectrum.reshape(128, 2, 3, 64)
    coupled = jnp.stack([jnp.stack([kernel[source][target] for target in range(3)], axis=1) for source in range(3)], axis=1)
    forced = (coupled[:, None] * spec[:, :, None]).sum(axis=3) * scale
    forced = forced.reshape(128, 384)
    back = dft8_apply(forced, True)
    back = z_twiddle(back[:, :192], back[:, 192:], 1)
    re, im = combine_rows(matmul("kg,gc->kc", table, back), 1)
    back = jnp.concatenate([re, im], axis=1)
    returned = lax.all_to_all(back, "gz", split_axis=0, concat_axis=0, tiled=True)
    spatial = y_inverse(returned)
    spatial = twiddle(spatial, phase_cos, phase_sin)
    result = dft4_across(lax.all_gather(spatial, "gy", axis=0), gy_index, 1)
    return result


def solution(mesh):
    in_specs = (P(None, None, None, "gz", "gy"), P(), P())
    out_specs = P(None, None, None, "gz", "gy")
    return jax.shard_map(shards, mesh=mesh, in_specs=in_specs, out_specs=out_specs, check_vma=False)
```

```python
import math

import numpy as np

import jax
import jax.numpy as jnp
from jax import lax
from jax.sharding import PartitionSpec as P

NX = 2048
NY = 2048
NZ = 1024


highest = lax.Precision.HIGHEST


def partner_2(value, axis, stride):
    mask = 2**stride
    pairs = [(source, source ^ mask) for source in range(lax.axis_size(axis))]
    return lax.ppermute(value, axis, pairs)


def signed_wave(index, length):
    return jnp.where(index < length // 2, index, index - length).astype(jnp.float32) / length


def kernel_rows(kx_wave, ky_wave, kz_wave, eigenstrain, moduli):
    constants = moduli.reshape(3, 1, 1)
    stiff_a = constants[0]
    stiff_b = constants[1]
    shear = constants[2]
    strain = eigenstrain
    trace = strain[:, 0:1] + strain[:, 1:2] + strain[:, 2:3]
    stress = jnp.concatenate(
        [
            moduli[1:2] * trace + (moduli[0:1] - moduli[1:2]) * strain[:, 0:3],
            2.0 * moduli[2:3] * strain[:, 3:6],
        ],
        axis=1,
    )
    voigt = [[0, 5, 4], [5, 1, 3], [4, 3, 2]]
    energy = sum(
        (
            stress[:, None, voigt[first][second]] * strain[None, :, voigt[first][second]]
            for first in range(3)
            for second in range(3)
        )
    )
    width = kx_wave.shape[-1]
    constants = jnp.broadcast_to(moduli[:, None], (3, width))
    stress_b = jnp.broadcast_to(stress[:, :, None], (3, 6, width))
    energy = jnp.broadcast_to(energy[:, :, None], (3, 3, width))
    constants, stress_b, energy = lax.optimization_barrier((constants, stress_b, energy))
    stiff_a = constants[0]
    stiff_b = constants[1]
    shear = constants[2]
    square = kx_wave * kx_wave + ky_wave * ky_wave + kz_wave * kz_wave
    inside = square > 0.0
    inverse = lax.rsqrt(jnp.where(inside, square, 1.0))
    normal = [kx_wave * inverse, ky_wave * inverse, kz_wave * inverse]
    g_diag = [shear + (stiff_a - shear) * normal[axis_id] * normal[axis_id] for axis_id in range(3)]
    cross_coef = stiff_b + shear
    g_zero_one = cross_coef * normal[0] * normal[1]
    g_zero_two = cross_coef * normal[0] * normal[2]
    g_one_two = cross_coef * normal[1] * normal[2]
    cof_zz = g_diag[1] * g_diag[2] - g_one_two * g_one_two
    cof_zo = g_zero_two * g_one_two - g_zero_one * g_diag[2]
    cof_zt = g_zero_one * g_one_two - g_zero_two * g_diag[1]
    cof_oo = g_diag[0] * g_diag[2] - g_zero_two * g_zero_two
    cof_ot = g_zero_one * g_zero_two - g_diag[0] * g_one_two
    cof_tt = g_diag[0] * g_diag[1] - g_zero_one * g_zero_one
    determinant = g_diag[0] * cof_zz + g_zero_one * cof_zo + g_zero_two * cof_zt
    recip = 1.0 / determinant
    omega = [
        [cof_zz * recip, cof_zo * recip, cof_zt * recip],
        [cof_zo * recip, cof_oo * recip, cof_ot * recip],
        [cof_zt * recip, cof_ot * recip, cof_tt * recip],
    ]
    traction = []
    for variant in range(3):
        traction.append(
            [
                sum((stress_b[variant, voigt[first][second]] * normal[second] for second in range(3)))
                for first in range(3)
            ]
        )
    response = []
    for variant in range(3):
        response.append(
            [
                sum((omega[first][second] * traction[variant][second] for second in range(3)))
                for first in range(3)
            ]
        )
    kernel = []
    for source in range(3):
        kernel_row = []
        for target in range(3):
            coupling = sum(
                (traction[source][first] * response[target][first] for first in range(3))
            )
            kernel_row.append(jnp.where(inside, energy[source, target] - coupling, 0.0))
        kernel.append(kernel_row)
    return kernel


def cos_sin(numer, length):
    angle = (2.0 * math.pi / length) * (numer % length).astype(jnp.float32)
    return (jnp.cos(angle), jnp.sin(angle))


def np_cos_sin(numer, length):
    angle = (2.0 * np.pi / length) * (numer % length).astype(np.float64)
    return (np.cos(angle).astype(np.float32), np.sin(angle).astype(np.float32))


def stacked_table(length):
    index = np.arange(length)
    cosine, sine = np_cos_sin(np.outer(index, index), length)
    return np.concatenate([cosine, sine], axis=0)


def block_dft8():
    size = 192
    rows_idx = lax.broadcasted_iota(jnp.int32, (size, size), 0)
    cols_idx = lax.broadcasted_iota(jnp.int32, (size, size), 1)
    same = (rows_idx // 32 == cols_idx // 32) & (rows_idx % 4 == cols_idx % 4)
    cosine, sine = cos_sin(((rows_idx // 4) % 8) * ((cols_idx // 4) % 8), 8)
    cosine = jnp.where(same, cosine, 0.0)
    sine = jnp.where(same, sine, 0.0)
    top = jnp.concatenate([cosine, -sine], axis=1)
    bottom = jnp.concatenate([sine, cosine], axis=1)
    return jnp.concatenate([top, bottom], axis=0)


def dft8_parts(inverse):
    rows = lax.broadcasted_iota(jnp.int32, (384, 384), 0)
    cols = lax.broadcasted_iota(jnp.int32, (384, 384), 1)
    if inverse:
        rows, cols = cols, rows
    inner_r = rows % 192
    inner_c = cols % 192
    same = (inner_r // 32 == inner_c // 32) & (inner_r % 4 == inner_c % 4)
    m = (((inner_r // 4) % 8) * ((inner_c // 4) % 8)) % 8

    def pick(plus, minus):
        hit_plus = (m == plus[0]) | (m == plus[-1])
        hit_minus = (m == minus[0]) | (m == minus[-1])
        return jnp.where(hit_plus, 1.0, jnp.where(hit_minus, -1.0, 0.0))

    diag = rows // 192 == cols // 192
    sign = jnp.where(rows // 192 == 0, -1.0, 1.0)
    unit = jnp.where(same, jnp.where(diag, pick((0,), (4,)), sign * pick((2,), (6,))), 0.0)
    half = jnp.where(same, jnp.where(diag, pick((1, 7), (3, 5)), sign * pick((1, 3), (5, 7))), 0.0)
    return jnp.concatenate([unit, half], axis=1).astype(jnp.bfloat16)


def dft8_apply(values, inverse):
    table = dft8_parts(inverse)
    first = lax.reduce_precision(values, exponent_bits=8, mantissa_bits=7)
    rest = values - first
    second = lax.reduce_precision(rest, exponent_bits=8, mantissa_bits=7)
    third = rest - second
    parts = jnp.concatenate([first, second, third], axis=0).astype(jnp.bfloat16)
    product = jnp.dot(parts, table, preferred_element_type=jnp.float32)
    summed = product[:128] + product[128:256] + product[256:]
    return summed[:, :384] + np.float32(math.sqrt(0.5)) * summed[:, 384:]


def block_dft8_np():
    size = 192
    rows_idx = np.arange(size)[:, None]
    cols_idx = np.arange(size)[None, :]
    same = (rows_idx // 32 == cols_idx // 32) & (rows_idx % 4 == cols_idx % 4)
    cosine, sine = np_cos_sin(((rows_idx // 4) % 8) * ((cols_idx // 4) % 8), 8)
    cosine = np.where(same, cosine, 0.0).astype(np.float32)
    sine = np.where(same, sine, 0.0).astype(np.float32)
    top = np.concatenate([cosine, -sine], axis=1)
    bottom = np.concatenate([sine, cosine], axis=1)
    return np.concatenate([top, bottom], axis=0)


def z_twiddle_table():
    rows_idx = lax.broadcasted_iota(jnp.int32, (128, 192), 0)
    cols_idx = lax.broadcasted_iota(jnp.int32, (128, 192), 1)
    return jnp.stack(cos_sin(rows_idx * ((cols_idx // 4) % 8), 1024))


def matmul(spec, left, right):
    return jnp.einsum(spec, left, right, precision=highest)


def combine_rows(product, sign):
    c_re = product[:128, :192]
    c_im = product[:128, 192:]
    s_re = product[128:, :192]
    s_im = product[128:, 192:]
    if sign < 0:
        return (c_re + s_im, c_im - s_re)
    return (c_re - s_im, c_im + s_re)


def twiddle(values, factor_cos, factor_sin):
    real_part = values[0] * factor_cos - values[1] * factor_sin
    imag_part = values[1] * factor_cos + values[0] * factor_sin
    return jnp.stack([real_part, imag_part])


def rotate_neg(values):
    return jnp.stack([values[1], -values[0]])


def rotate_pos(values):
    return jnp.stack([-values[1], values[0]])


def times_i(re, im, sign):
    return (-sign * im, sign * re)


def dft4(parts, sign):
    (r0, i0), (r1, i1), (r2, i2), (r3, i3) = parts
    ar, ai = r0 + r2, i0 + i2
    br, bi = r0 - r2, i0 - i2
    cr, ci = r1 + r3, i1 + i3
    dr, di = times_i(r1 - r3, i1 - i3, sign)
    return [(ar + cr, ai + ci), (br + dr, bi + di), (ar - cr, ai - ci), (br - dr, bi - di)]


def dft4_across(gathered, index, sign):
    (r0, i0), (r1, i1), (r2, i2), (r3, i3) = [(gathered[g, 0], gathered[g, 1]) for g in range(4)]
    ar, ai = r0 + r2, i0 + i2
    br, bi = r0 - r2, i0 - i2
    cr, ci = r1 + r3, i1 + i3
    dr, di = times_i(r1 - r3, i1 - i3, sign)
    choices = [(ar + cr, ai + ci), (br + dr, bi + di), (ar - cr, ai - ci), (br - dr, bi - di)]
    real_part = choices[3][0]
    imag_part = choices[3][1]
    for position in (2, 1, 0):
        real_part = jnp.where(index == position, choices[position][0], real_part)
        imag_part = jnp.where(index == position, choices[position][1], imag_part)
    return jnp.stack([real_part, imag_part])


def y_forward(spectral):
    parts = [(spectral[0, ..., 128 * a:128 * a + 128], spectral[1, ..., 128 * a:128 * a + 128]) for a in range(4)]
    mixed = dft4(parts, -1)
    lanes = lax.broadcasted_iota(jnp.int32, (128,), 0)
    out = []
    for k1 in range(4):
        tw_cos, tw_sin = cos_sin(lanes * k1, 512)
        re, im = mixed[k1]
        out.append(jnp.stack([re * tw_cos + im * tw_sin, im * tw_cos - re * tw_sin]))
    stacked = jnp.stack(out, axis=-2).reshape(384, 128)
    product = matmul("kb,rb->kr", stacked_table(128), stacked)
    re, im = combine_rows(product, -1)
    return jnp.concatenate([re, im], axis=1)


def y_inverse(returned):
    product = matmul("kr,bk->rb", returned, stacked_table(128))
    c_re = product[:192, :128]
    s_re = product[:192, 128:]
    c_im = product[192:, :128]
    s_im = product[192:, 128:]
    re = (c_re - s_im).reshape(3, 2, 8, 4, 128)
    im = (c_im + s_re).reshape(3, 2, 8, 4, 128)
    k1 = lax.broadcasted_iota(jnp.int32, (4, 128), 0)
    lanes = lax.broadcasted_iota(jnp.int32, (4, 128), 1)
    tw_cos, tw_sin = cos_sin(lanes * k1, 512)
    turned_re = re * tw_cos - im * tw_sin
    turned_im = im * tw_cos + re * tw_sin
    parts = [(turned_re[..., k, :], turned_im[..., k, :]) for k in range(4)]
    mixed = dft4(parts, 1)
    real_part = jnp.concatenate([m[0] for m in mixed], axis=-1)
    imag_part = jnp.concatenate([m[1] for m in mixed], axis=-1)
    return jnp.stack([real_part, imag_part])


def z_twiddle(re, im, sign):
    table = z_twiddle_table()
    tw_cos = table[0]
    tw_sin = sign * table[1]
    return jnp.concatenate([re * tw_cos - im * tw_sin, im * tw_cos + re * tw_sin], axis=1)


def shards(fields, eigenstrain, moduli):
    gy_count = lax.axis_size("gy")
    gy_index = lax.axis_index("gy")
    gz_index = lax.axis_index("gz")
    y_local = fields.shape[4]
    positions = lax.broadcasted_iota(jnp.int32, (y_local,), 0)
    spectral = dft4_across(lax.all_gather(fields, "gy", axis=0), gy_index, -1)
    residue = gy_index
    angle = 2.0 * math.pi / NY * (positions * residue % NY).astype(jnp.float32)
    phase_cos = jnp.cos(angle)
    phase_sin = jnp.sin(angle)
    spectral = twiddle(spectral, phase_cos, -phase_sin)
    slabs = y_forward(spectral)
    pencils = lax.all_to_all(slabs, "gz", split_axis=0, concat_axis=0, tiled=True)
    table = stacked_table(128)
    re, im = combine_rows(matmul("kg,gc->kc", table, pencils), -1)
    spectrum = dft8_apply(z_twiddle(re, im, -1), False)
    rows_idx = lax.broadcasted_iota(jnp.int32, (128, 64), 0)
    cols_idx = lax.broadcasted_iota(jnp.int32, (128, 64), 1)
    plane = cols_idx // 32
    kz_index = rows_idx + 128 * ((cols_idx // 4) % 8)
    ky_index = residue + gy_count * (cols_idx % 4 + 4 * gz_index)
    kx_wave = plane.astype(jnp.float32) / NX
    ky_wave = signed_wave(ky_index, NY)
    kz_wave = signed_wave(kz_index, NZ)
    kernel = kernel_rows(kx_wave, ky_wave, kz_wave, eigenstrain, moduli)
    scale = 1.0 / (NY * NZ)
    spec = spectrum.reshape(128, 2, 3, 64)
    coupled = jnp.stack([jnp.stack([kernel[source][target] for target in range(3)], axis=1) for source in range(3)], axis=1)
    forced = (coupled[:, None] * spec[:, :, None]).sum(axis=3) * scale
    forced = forced.reshape(128, 384)
    back = dft8_apply(forced, True)
    back = z_twiddle(back[:, :192], back[:, 192:], 1)
    re, im = combine_rows(matmul("kg,gc->kc", table, back), 1)
    back = jnp.concatenate([re, im], axis=1)
    returned = lax.all_to_all(back, "gz", split_axis=0, concat_axis=0, tiled=True)
    spatial = y_inverse(returned)
    spatial = twiddle(spatial, phase_cos, phase_sin)
    result = dft4_across(lax.all_gather(spatial, "gy", axis=0), gy_index, 1)
    return result


def solution(mesh):
    in_specs = (P(None, None, None, "gz", "gy"), P(), P())
    out_specs = P(None, None, None, "gz", "gy")
    return jax.shard_map(shards, mesh=mesh, in_specs=in_specs, out_specs=out_specs, check_vma=False)
```

```python
import math

import numpy as np

import jax
import jax.numpy as jnp
from jax import lax
from jax.sharding import PartitionSpec as P

NX = 2048
NY = 2048
NZ = 1024


highest = lax.Precision.HIGHEST


def partner_2(value, axis, stride):
    mask = 2**stride
    pairs = [(source, source ^ mask) for source in range(lax.axis_size(axis))]
    return lax.ppermute(value, axis, pairs)


def signed_wave(index, length):
    return jnp.where(index < length // 2, index, index - length).astype(jnp.float32) / length


def kernel_rows(kx_wave, ky_wave, kz_wave, eigenstrain, moduli):
    constants = moduli.reshape(3, 1, 1)
    stiff_a = constants[0]
    stiff_b = constants[1]
    shear = constants[2]
    strain = eigenstrain
    trace = strain[:, 0:1] + strain[:, 1:2] + strain[:, 2:3]
    stress = jnp.concatenate(
        [
            moduli[1:2] * trace + (moduli[0:1] - moduli[1:2]) * strain[:, 0:3],
            2.0 * moduli[2:3] * strain[:, 3:6],
        ],
        axis=1,
    )
    voigt = [[0, 5, 4], [5, 1, 3], [4, 3, 2]]
    energy = sum(
        (
            stress[:, None, voigt[first][second]] * strain[None, :, voigt[first][second]]
            for first in range(3)
            for second in range(3)
        )
    )
    width = kx_wave.shape[-1]
    constants = jnp.broadcast_to(moduli[:, None], (3, width))
    stress_b = jnp.broadcast_to(stress[:, :, None], (3, 6, width))
    energy = jnp.broadcast_to(energy[:, :, None], (3, 3, width))
    constants, stress_b, energy = lax.optimization_barrier((constants, stress_b, energy))
    stiff_a = constants[0]
    stiff_b = constants[1]
    shear = constants[2]
    square = kx_wave * kx_wave + ky_wave * ky_wave + kz_wave * kz_wave
    inside = square > 0.0
    inverse = lax.rsqrt(jnp.where(inside, square, 1.0))
    normal = [kx_wave * inverse, ky_wave * inverse, kz_wave * inverse]
    g_diag = [shear + (stiff_a - shear) * normal[axis_id] * normal[axis_id] for axis_id in range(3)]
    cross_coef = stiff_b + shear
    g_zero_one = cross_coef * normal[0] * normal[1]
    g_zero_two = cross_coef * normal[0] * normal[2]
    g_one_two = cross_coef * normal[1] * normal[2]
    cof_zz = g_diag[1] * g_diag[2] - g_one_two * g_one_two
    cof_zo = g_zero_two * g_one_two - g_zero_one * g_diag[2]
    cof_zt = g_zero_one * g_one_two - g_zero_two * g_diag[1]
    cof_oo = g_diag[0] * g_diag[2] - g_zero_two * g_zero_two
    cof_ot = g_zero_one * g_zero_two - g_diag[0] * g_one_two
    cof_tt = g_diag[0] * g_diag[1] - g_zero_one * g_zero_one
    determinant = g_diag[0] * cof_zz + g_zero_one * cof_zo + g_zero_two * cof_zt
    recip = 1.0 / determinant
    omega = [
        [cof_zz * recip, cof_zo * recip, cof_zt * recip],
        [cof_zo * recip, cof_oo * recip, cof_ot * recip],
        [cof_zt * recip, cof_ot * recip, cof_tt * recip],
    ]
    traction = []
    for variant in range(3):
        traction.append(
            [
                sum((stress_b[variant, voigt[first][second]] * normal[second] for second in range(3)))
                for first in range(3)
            ]
        )
    response = []
    for variant in range(3):
        response.append(
            [
                sum((omega[first][second] * traction[variant][second] for second in range(3)))
                for first in range(3)
            ]
        )
    kernel = []
    for source in range(3):
        kernel_row = []
        for target in range(3):
            coupling = sum(
                (traction[source][first] * response[target][first] for first in range(3))
            )
            kernel_row.append(jnp.where(inside, energy[source, target] - coupling, 0.0))
        kernel.append(kernel_row)
    return kernel


def cos_sin(numer, length):
    angle = (2.0 * math.pi / length) * (numer % length).astype(jnp.float32)
    return (jnp.cos(angle), jnp.sin(angle))


def np_cos_sin(numer, length):
    angle = (2.0 * np.pi / length) * (numer % length).astype(np.float64)
    return (np.cos(angle).astype(np.float32), np.sin(angle).astype(np.float32))


def stacked_table(length):
    index = np.arange(length)
    cosine, sine = np_cos_sin(np.outer(index, index), length)
    return np.concatenate([cosine, sine], axis=0)


def block_dft8():
    size = 192
    rows_idx = lax.broadcasted_iota(jnp.int32, (size, size), 0)
    cols_idx = lax.broadcasted_iota(jnp.int32, (size, size), 1)
    same = (rows_idx // 32 == cols_idx // 32) & (rows_idx % 4 == cols_idx % 4)
    cosine, sine = cos_sin(((rows_idx // 4) % 8) * ((cols_idx // 4) % 8), 8)
    cosine = jnp.where(same, cosine, 0.0)
    sine = jnp.where(same, sine, 0.0)
    top = jnp.concatenate([cosine, -sine], axis=1)
    bottom = jnp.concatenate([sine, cosine], axis=1)
    return jnp.concatenate([top, bottom], axis=0)


def dft8_parts(inverse):
    rows = lax.broadcasted_iota(jnp.int32, (384, 384), 0)
    cols = lax.broadcasted_iota(jnp.int32, (384, 384), 1)
    if inverse:
        rows, cols = cols, rows
    inner_r = rows % 192
    inner_c = cols % 192
    same = (inner_r // 32 == inner_c // 32) & (inner_r % 4 == inner_c % 4)
    m = (((inner_r // 4) % 8) * ((inner_c // 4) % 8)) % 8

    def pick(plus, minus):
        hit_plus = (m == plus[0]) | (m == plus[-1])
        hit_minus = (m == minus[0]) | (m == minus[-1])
        return jnp.where(hit_plus, 1.0, jnp.where(hit_minus, -1.0, 0.0))

    diag = rows // 192 == cols // 192
    sign = jnp.where(rows // 192 == 0, -1.0, 1.0)
    unit = jnp.where(same, jnp.where(diag, pick((0,), (4,)), sign * pick((2,), (6,))), 0.0)
    half = jnp.where(same, jnp.where(diag, pick((1, 7), (3, 5)), sign * pick((1, 3), (5, 7))), 0.0)
    return jnp.concatenate([unit, half], axis=1).astype(jnp.bfloat16)


def dft8_apply(values, inverse):
    table = dft8_parts(inverse)
    first = lax.reduce_precision(values, exponent_bits=8, mantissa_bits=7)
    rest = values - first
    second = lax.reduce_precision(rest, exponent_bits=8, mantissa_bits=7)
    third = rest - second
    parts = jnp.concatenate([first, second, third], axis=0).astype(jnp.bfloat16)
    product = jnp.dot(parts, table, preferred_element_type=jnp.float32)
    summed = product[:128] + product[128:256] + product[256:]
    return summed[:, :384] + np.float32(math.sqrt(0.5)) * summed[:, 384:]


def block_dft8_np():
    size = 192
    rows_idx = np.arange(size)[:, None]
    cols_idx = np.arange(size)[None, :]
    same = (rows_idx // 32 == cols_idx // 32) & (rows_idx % 4 == cols_idx % 4)
    cosine, sine = np_cos_sin(((rows_idx // 4) % 8) * ((cols_idx // 4) % 8), 8)
    cosine = np.where(same, cosine, 0.0).astype(np.float32)
    sine = np.where(same, sine, 0.0).astype(np.float32)
    top = np.concatenate([cosine, -sine], axis=1)
    bottom = np.concatenate([sine, cosine], axis=1)
    return np.concatenate([top, bottom], axis=0)


def z_twiddle_table():
    rows_idx = lax.broadcasted_iota(jnp.int32, (128, 192), 0)
    cols_idx = lax.broadcasted_iota(jnp.int32, (128, 192), 1)
    return jnp.stack(cos_sin(rows_idx * ((cols_idx // 4) % 8), 1024))


def matmul(spec, left, right):
    return jnp.einsum(spec, left, right, precision=highest)


def combine_rows(product, sign):
    c_re = product[:128, :192]
    c_im = product[:128, 192:]
    s_re = product[128:, :192]
    s_im = product[128:, 192:]
    if sign < 0:
        return (c_re + s_im, c_im - s_re)
    return (c_re - s_im, c_im + s_re)


def twiddle(values, factor_cos, factor_sin):
    real_part = values[0] * factor_cos - values[1] * factor_sin
    imag_part = values[1] * factor_cos + values[0] * factor_sin
    return jnp.stack([real_part, imag_part])


def rotate_neg(values):
    return jnp.stack([values[1], -values[0]])


def rotate_pos(values):
    return jnp.stack([-values[1], values[0]])


def times_i(re, im, sign):
    return (-sign * im, sign * re)


def dft4(parts, sign):
    (r0, i0), (r1, i1), (r2, i2), (r3, i3) = parts
    ar, ai = r0 + r2, i0 + i2
    br, bi = r0 - r2, i0 - i2
    cr, ci = r1 + r3, i1 + i3
    dr, di = times_i(r1 - r3, i1 - i3, sign)
    return [(ar + cr, ai + ci), (br + dr, bi + di), (ar - cr, ai - ci), (br - dr, bi - di)]


def dft4_across(gathered, index, sign):
    (r0, i0), (r1, i1), (r2, i2), (r3, i3) = [(gathered[g, 0], gathered[g, 1]) for g in range(4)]
    ar, ai = r0 + r2, i0 + i2
    br, bi = r0 - r2, i0 - i2
    cr, ci = r1 + r3, i1 + i3
    dr, di = times_i(r1 - r3, i1 - i3, sign)
    choices = [(ar + cr, ai + ci), (br + dr, bi + di), (ar - cr, ai - ci), (br - dr, bi - di)]
    real_part = choices[3][0]
    imag_part = choices[3][1]
    for position in (2, 1, 0):
        real_part = jnp.where(index == position, choices[position][0], real_part)
        imag_part = jnp.where(index == position, choices[position][1], imag_part)
    return jnp.stack([real_part, imag_part])


def y_forward(spectral):
    parts = [(spectral[0, ..., 128 * a:128 * a + 128], spectral[1, ..., 128 * a:128 * a + 128]) for a in range(4)]
    mixed = dft4(parts, -1)
    re = jnp.stack([m[0] for m in mixed], axis=-2)
    im = jnp.stack([m[1] for m in mixed], axis=-2)
    k1 = lax.broadcasted_iota(jnp.int32, (4, 128), 0)
    lanes = lax.broadcasted_iota(jnp.int32, (4, 128), 1)
    tw_cos, tw_sin = cos_sin(lanes * k1, 512)
    stacked = jnp.stack([re * tw_cos + im * tw_sin, im * tw_cos - re * tw_sin]).reshape(384, 128)
    product = matmul("kb,rb->kr", stacked_table(128), stacked)
    re, im = combine_rows(product, -1)
    return jnp.concatenate([re, im], axis=1)


def y_inverse(returned):
    product = matmul("kr,bk->rb", returned, stacked_table(128))
    c_re = product[:192, :128]
    s_re = product[:192, 128:]
    c_im = product[192:, :128]
    s_im = product[192:, 128:]
    re = (c_re - s_im).reshape(3, 2, 8, 4, 128)
    im = (c_im + s_re).reshape(3, 2, 8, 4, 128)
    k1 = lax.broadcasted_iota(jnp.int32, (4, 128), 0)
    lanes = lax.broadcasted_iota(jnp.int32, (4, 128), 1)
    tw_cos, tw_sin = cos_sin(lanes * k1, 512)
    turned_re = re * tw_cos - im * tw_sin
    turned_im = im * tw_cos + re * tw_sin
    parts = [(turned_re[..., k, :], turned_im[..., k, :]) for k in range(4)]
    mixed = dft4(parts, 1)
    real_part = jnp.concatenate([m[0] for m in mixed], axis=-1)
    imag_part = jnp.concatenate([m[1] for m in mixed], axis=-1)
    return jnp.stack([real_part, imag_part])


def z_twiddle(re, im, sign):
    table = z_twiddle_table()
    tw_cos = table[0]
    tw_sin = sign * table[1]
    return jnp.concatenate([re * tw_cos - im * tw_sin, im * tw_cos + re * tw_sin], axis=1)


def shards(fields, eigenstrain, moduli):
    gy_count = lax.axis_size("gy")
    gy_index = lax.axis_index("gy")
    gz_index = lax.axis_index("gz")
    y_local = fields.shape[4]
    positions = lax.broadcasted_iota(jnp.int32, (y_local,), 0)
    spectral = dft4_across(lax.all_gather(fields, "gy", axis=0), gy_index, -1)
    residue = gy_index
    angle = 2.0 * math.pi / NY * (positions * residue % NY).astype(jnp.float32)
    phase_cos = jnp.cos(angle)
    phase_sin = jnp.sin(angle)
    spectral = twiddle(spectral, phase_cos, -phase_sin)
    slabs = y_forward(spectral)
    pencils = lax.all_to_all(slabs, "gz", split_axis=0, concat_axis=0, tiled=True)
    table = stacked_table(128)
    re, im = combine_rows(matmul("kg,gc->kc", table, pencils), -1)
    spectrum = dft8_apply(z_twiddle(re, im, -1), False)
    rows_idx = lax.broadcasted_iota(jnp.int32, (128, 64), 0)
    cols_idx = lax.broadcasted_iota(jnp.int32, (128, 64), 1)
    plane = cols_idx // 32
    kz_index = rows_idx + 128 * ((cols_idx // 4) % 8)
    ky_index = residue + gy_count * (cols_idx % 4 + 4 * gz_index)
    kx_wave = plane.astype(jnp.float32) / NX
    ky_wave = signed_wave(ky_index, NY)
    kz_wave = signed_wave(kz_index, NZ)
    kernel = kernel_rows(kx_wave, ky_wave, kz_wave, eigenstrain, moduli)
    scale = 1.0 / (NY * NZ)
    spec = spectrum.reshape(128, 2, 3, 64)
    coupled = jnp.stack([jnp.stack([kernel[source][target] for target in range(3)], axis=1) for source in range(3)], axis=1)
    forced = (coupled[:, None] * spec[:, :, None]).sum(axis=3) * scale
    forced = forced.reshape(128, 384)
    back = dft8_apply(forced, True)
    back = z_twiddle(back[:, :192], back[:, 192:], 1)
    re, im = combine_rows(matmul("kg,gc->kc", table, back), 1)
    back = jnp.concatenate([re, im], axis=1)
    returned = lax.all_to_all(back, "gz", split_axis=0, concat_axis=0, tiled=True)
    spatial = y_inverse(returned)
    spatial = twiddle(spatial, phase_cos, phase_sin)
    result = dft4_across(lax.all_gather(spatial, "gy", axis=0), gy_index, 1)
    return result


def solution(mesh):
    in_specs = (P(None, None, None, "gz", "gy"), P(), P())
    out_specs = P(None, None, None, "gz", "gy")
    return jax.shard_map(shards, mesh=mesh, in_specs=in_specs, out_specs=out_specs, check_vma=False)
```
